256 devices in a mesh: gx: 16 (over x_hi, y, core), gy: 16 (over z, x_lo).
Axes of the slice: x: 4 (x_hi: 2, x_lo: 2; x = x_hi * 2 + x_lo), y: 4, z: 8, core: 2. Of those that a mesh axis runs over, the one named last changes fastest.
Arguments:
- tracers: float32 [2, 16, 512, 2048], P(None, None, 'gx', 'gy'), may hold values from 0.1 to 10
- wind_x: float32 [16, 512, 2048], P(None, 'gx', 'gy'), may hold values from -0.45 to 0.45
- wind_y: float32 [16, 512, 2048], P(None, 'gx', 'gy'), may hold values from -0.45 to 0.45
- kdiff: float32 [15, 512, 2048], P(None, 'gx', 'gy'), may hold values from 0.05 to 5
- rate: float32 [512, 2048], P('gx', 'gy'), may hold values from 0.02 to 0.5
- seg_blocks: float32 [8192, 2048], P(('gx', 'gy')), may hold values from 0.2 to 5
- seg_target: int32 [8192], P(('gx', 'gy')), may hold values from 0 to 15, as said below
- seg_row: int32 [8192], P(('gx', 'gy')), may hold values from 0 to 1
- seg_top: int32 [8192], P(('gx', 'gy')), may hold values from 1 to 16
Outputs:
- tracers_out: float32 [2, 16, 512, 2048], P(None, None, 'gx', 'gy')
The draws below stay inside these ranges and needn't reach their ends.
Inputs may be any that keep to these rules, and one draw needn't show every extreme that they name: `seg_target`: within the segments of one tile's list, no tile column is named by more than 8 segments; in every row of tiles one column is named by exactly 8 segments of every list of that row.
All inputs are finite; a program needn't handle non-finite values.
Results may differ from the reference program's by a relative error of at most 0.0001.
Values sent between devices are 32-bit elements; how exact they have to be, the bound alone decides.
No kernel may reach another device: no remote copies, remote signals or barrier semaphores. Data moves between devices by JAX's collectives and lax.ppermute only.
A program may use at most 64 MiB of HBM per device.

```python
import math
import jax
import jax.numpy as jnp
from jax import lax

CY = 128
LEV = 16
STEPS = 4
PR = 16
SEG_DEV = 32
CAP = 8
TILES_X = 16
TILES_Y = 16
NX = 512
NY = 2048
RB = 2
BLOCK = 2048
SEGS = 8192


def draw_seg_target(key, part):
    key_hot, key_dev = jax.random.split(key)
    hot = jax.random.randint(key_hot, (TILES_X,), 0, TILES_Y)
    dev_keys = jax.random.split(key_dev, TILES_X * TILES_Y)

    def one_list(dev_key):
        key_fill, key_order = jax.random.split(dev_key)
        others = jax.random.permutation(key_fill, (TILES_Y - 1) * CAP)[:SEG_DEV - CAP] // CAP
        offsets = jnp.concatenate([jnp.zeros((CAP,), jnp.int32), 1 + others.astype(jnp.int32)])
        order = jax.random.permutation(key_order, SEG_DEV)
        return offsets[order]
    offsets = jax.vmap(one_list)(dev_keys).reshape(TILES_X, TILES_Y, SEG_DEV)
    target = (hot[:, None, None].astype(jnp.int32) + offsets) % TILES_Y
    return target.reshape(-1).astype(jnp.int32)


def with_ends(entries, rng, smallest, largest):
    spot = [jax.random.randint(jax.random.fold_in(rng, axis), (), 0, length) for axis, length in enumerate(entries.shape)]
    widest = entries.shape.index(max(entries.shape))
    neighbour = spot[:widest] + [(spot[widest] + 1) % entries.shape[widest]] + spot[widest + 1:]
    return entries.at[tuple(spot)].set(smallest).at[tuple(neighbour)].set(largest)


def block_levels(rng, shape, cuts, least, largest):
    level, own = 1.0, jax.random.fold_in(rng, 6)
    for position, shards_of in cuts:
        steps = jnp.exp(jax.random.uniform(jax.random.fold_in(own, position), (shards_of,), jnp.float32, least / len(cuts), largest / len(cuts)))
        level = level * jnp.repeat(steps, shape[position] // shards_of).reshape([-1 if axis == position else 1 for axis in range(len(shape))])
    return level


def setup_inputs(seed: int = 0) -> dict:
    key_list = jax.random.split(jax.random.key(seed), 10)
    tracers = jnp.clip(jnp.exp(math.log(10.0) - 4.6051702 * jax.random.uniform(key_list[0], (2, LEV, NX, NY), jnp.float32) ** block_levels(key_list[0], (2, LEV, NX, NY), ((2, 16), (3, 16)), -0.2, 0.2)), 0.1, 10.0)
    wind_x = jnp.clip(jax.random.uniform(key_list[1], (LEV, NX, NY), jnp.float32, -0.45, 0.45) * block_levels(key_list[1], (LEV, NX, NY), ((1, 16), (2, 16)), -0.4, 0.0), -0.45, 0.45)
    wind_y = jnp.clip(jax.random.uniform(key_list[2], (LEV, NX, NY), jnp.float32, -0.45, 0.45) * block_levels(key_list[2], (LEV, NX, NY), ((1, 16), (2, 16)), -0.4, 0.0), -0.45, 0.45)
    kdiff = jnp.clip(jnp.exp(math.log(5.0) - 4.6051702 * jax.random.uniform(key_list[3], (LEV - 1, NX, NY), jnp.float32) ** block_levels(key_list[3], (LEV - 1, NX, NY), ((1, 16), (2, 16)), -0.2, 0.2)), 0.05, 5.0)
    rate = jnp.clip(jnp.exp(math.log(0.5) - 3.218876 * jax.random.uniform(key_list[4], (NX, NY), jnp.float32) ** block_levels(key_list[4], (NX, NY), ((0, 16), (1, 16)), -0.2, 0.2)), 0.02, 0.5)
    seg_blocks = jnp.clip(jnp.exp(math.log(5.0) - 3.218876 * jax.random.uniform(key_list[5], (SEGS, BLOCK), jnp.float32) ** block_levels(key_list[5], (SEGS, BLOCK), ((0, 256),), -0.2, 0.2)), 0.2, 5.0)
    seg_target = draw_seg_target(jax.random.fold_in(key_list[9], 71), 0)
    seg_row = with_ends(jax.random.randint(key_list[7], (SEGS,), 0, RB), jax.random.fold_in(key_list[7], 1), 0, RB - 1).astype(jnp.int32)
    seg_top = with_ends(jax.random.randint(key_list[8], (SEGS,), 1, LEV + 1), jax.random.fold_in(key_list[8], 1), 1, LEV).astype(jnp.int32)
    return {"tracers": tracers, "wind_x": wind_x, "wind_y": wind_y, "kdiff": kdiff, "rate": rate, "seg_blocks": seg_blocks, "seg_target": seg_target, "seg_row": seg_row, "seg_top": seg_top}


def thomas_factor(kdiff):
    levels = kdiff.shape[0] + 1
    lower = []
    upper = []
    diag = []
    for l in range(levels):
        d_here = jnp.ones_like(kdiff[0])
        if l >= 1:
            d_here = d_here + kdiff[l - 1]
            lower.append(-kdiff[l - 1])
        else:
            lower.append(jnp.zeros_like(kdiff[0]))
        if l < levels - 1:
            d_here = d_here + kdiff[l]
            upper.append(-kdiff[l])
        else:
            upper.append(jnp.zeros_like(kdiff[0]))
        diag.append(d_here)
    inverse = []
    sweep = []
    for l in range(levels):
        if l == 0:
            denom = diag[0]
        else:
            denom = diag[l] - lower[l] * sweep[l - 1]
        inv_here = 1.0 / denom
        inverse.append(inv_here)
        sweep.append(upper[l] * inv_here)
    return lower, inverse, sweep


def thomas_solve(rhs, factors):
    lower, inverse, sweep = factors
    levels = len(inverse)
    forward = []
    for l in range(levels):
        if l == 0:
            forward.append(rhs[:, 0] * inverse[0])
        else:
            forward.append((rhs[:, l] - lower[l] * forward[l - 1]) * inverse[l])
    result = [None] * levels
    result[levels - 1] = forward[levels - 1]
    for l in range(levels - 2, -1, -1):
        result[l] = forward[l] - sweep[l] * result[l + 1]
    return jnp.stack(result, axis=1)


def advect(field, wind_x, wind_y):
    zero_row = jnp.zeros_like(field[:, :, :1, :])
    ahead_x = jnp.concatenate([field[:, :, 1:, :], zero_row], axis=2)
    flux_x = jnp.maximum(wind_x, 0.0) * field + jnp.minimum(wind_x, 0.0) * ahead_x
    before_x = jnp.concatenate([jnp.zeros_like(flux_x[:, :, :1, :]), flux_x[:, :, :-1, :]], axis=2)
    zero_col = jnp.zeros_like(field[:, :, :, :1])
    ahead_y = jnp.concatenate([field[:, :, :, 1:], zero_col], axis=3)
    flux_y = jnp.maximum(wind_y, 0.0) * field + jnp.minimum(wind_y, 0.0) * ahead_y
    before_y = jnp.concatenate([jnp.zeros_like(flux_y[:, :, :, :1]), flux_y[:, :, :, :-1]], axis=3)
    return field - (flux_x - before_x) - (flux_y - before_y)


def reference(tracers, wind_x, wind_y, kdiff, rate, seg_blocks, seg_target, seg_row, seg_top):
    blocks = seg_blocks.reshape(SEGS, PR, CY)
    tile_row = (jnp.arange(SEGS, dtype=jnp.int32) // (SEG_DEV * TILES_Y)).astype(jnp.int32)
    top_f = seg_top.astype(jnp.float32)
    levels = jnp.arange(LEV, dtype=jnp.float32)
    weight = jnp.where(levels[None, :] < top_f[:, None], 1.0 / top_f[:, None], jnp.float32(0.0))

    def one_level(level_w):
        grid = jnp.zeros((TILES_X, RB, TILES_Y, PR, CY), jnp.float32)
        grid = grid.at[tile_row, seg_row.astype(jnp.int32), seg_target.astype(jnp.int32)].add(level_w[:, None, None] * blocks)
        return grid.transpose(0, 1, 3, 2, 4).reshape(NX, NY)

    injection = lax.map(one_level, weight.T)
    keep = 1.0 - jnp.exp(-rate)
    factors = thomas_factor(kdiff)
    field = tracers
    for step in range(STEPS):
        advected = advect(field, wind_x, wind_y)
        so2 = advected[0] + injection
        loss = so2 * keep
        converted = jnp.stack([so2 - loss, advected[1] + 1.5 * loss])
        field = thomas_solve(converted, factors)
    return field
```

```python
import jax
import jax.numpy as jnp
from jax import lax
from jax.sharding import PartitionSpec as P

LEV = 16
STEPS = 4
PR = 16
CAP = 8
HALO = STEPS


def from_behind(value, axis, steps):
    count = lax.axis_size(axis)
    initial, last = (max(0, -steps), min(count, count - steps))
    return lax.ppermute(value, axis, [(source, source + steps) for source in range(initial, last)])


def from_corner(value, dx, dy):
    nx = lax.axis_size("gx")
    ny = lax.axis_size("gy")
    pairs = []
    for i in range(nx):
        for j in range(ny):
            ti, tj = i + dx, j + dy
            if 0 <= ti < nx and 0 <= tj < ny:
                pairs.append((i * ny + j, ti * ny + tj))
    return lax.ppermute(value, ("gx", "gy"), pairs)


def with_halo(a, h):
    c, r, w = a.shape
    top = from_behind(a[:, r - h:, :], "gx", 1)
    bottom = from_behind(a[:, :h, :], "gx", -1)
    left = from_behind(a[:, :, w - h:].reshape(c, r * h), "gy", 1).reshape(c, r, h)
    right = from_behind(a[:, :, :h].reshape(c, r * h), "gy", -1).reshape(c, r, h)
    tl = from_corner(a[:, r - h:, w - h:].reshape(c, h * h), 1, 1).reshape(c, h, h)
    tr = from_corner(a[:, r - h:, :h].reshape(c, h * h), 1, -1).reshape(c, h, h)
    bl = from_corner(a[:, :h, w - h:].reshape(c, h * h), -1, 1).reshape(c, h, h)
    br = from_corner(a[:, :h, :h].reshape(c, h * h), -1, -1).reshape(c, h, h)
    upper = jnp.concatenate([tl, top, tr], axis=2)
    middle = jnp.concatenate([left, a, right], axis=2)
    lower = jnp.concatenate([bl, bottom, br], axis=2)
    return jnp.concatenate([upper, middle, lower], axis=1)


def thomas_factor(kdiff):
    levels = kdiff.shape[0] + 1
    lower = []
    upper = []
    diag = []
    for l in range(levels):
        d_here = jnp.ones_like(kdiff[0])
        if l >= 1:
            d_here = d_here + kdiff[l - 1]
            lower.append(-kdiff[l - 1])
        else:
            lower.append(jnp.zeros_like(kdiff[0]))
        if l < levels - 1:
            d_here = d_here + kdiff[l]
            upper.append(-kdiff[l])
        else:
            upper.append(jnp.zeros_like(kdiff[0]))
        diag.append(d_here)
    inverse = []
    sweep = []
    for l in range(levels):
        if l == 0:
            denom = diag[0]
        else:
            denom = diag[l] - lower[l] * sweep[l - 1]
        inv_here = 1.0 / denom
        inverse.append(inv_here)
        sweep.append(upper[l] * inv_here)
    return (lower, inverse, sweep)


def thomas_solve(rhs, factors):
    lower, inverse, sweep = factors
    levels = len(inverse)
    forward = []
    for l in range(levels):
        if l == 0:
            forward.append(rhs[:, 0] * inverse[0])
        else:
            forward.append((rhs[:, l] - lower[l] * forward[l - 1]) * inverse[l])
    result = [None] * levels
    result[levels - 1] = forward[levels - 1]
    for l in range(levels - 2, -1, -1):
        result[l] = forward[l] - sweep[l] * result[l + 1]
    return jnp.stack(result, axis=1)


def upwind(courant, here, ahead):
    return jnp.maximum(courant, 0.0) * here + jnp.minimum(courant, 0.0) * ahead


def plume_matrix(blocks, row_f, top_f, positions):
    levels = jnp.arange(LEV, dtype=jnp.float32)
    weight = jnp.where(
        levels[None, :] < top_f[:, None], 1.0 / jnp.maximum(top_f, 1.0)[:, None], jnp.float32(0.0)
    )
    place = (row_f[:, None] == jnp.arange(positions, dtype=jnp.float32)[None, :]).astype(
        jnp.float32
    )
    mixed = (weight[:, :, None] * place[:, None, :]).reshape(blocks.shape[0], LEV * positions)
    return jnp.dot(
        mixed.T, blocks, precision=lax.Precision.HIGHEST, preferred_element_type=jnp.float32
    )


def advect_local(field, wind_x, wind_y):
    zero_row = jnp.zeros_like(field[:, :, :1, :])
    ahead_x = jnp.concatenate([field[:, :, 1:, :], zero_row], axis=2)
    flux_x = upwind(wind_x, field, ahead_x)
    before_x = jnp.concatenate([jnp.zeros_like(flux_x[:, :, :1, :]), flux_x[:, :, :-1, :]], axis=2)
    zero_col = jnp.zeros_like(field[:, :, :, :1])
    ahead_y = jnp.concatenate([field[:, :, :, 1:], zero_col], axis=3)
    flux_y = upwind(wind_y, field, ahead_y)
    before_y = jnp.concatenate([jnp.zeros_like(flux_y[:, :, :, :1]), flux_y[:, :, :, :-1]], axis=3)
    return field - (flux_x - before_x) - (flux_y - before_y)


def on_device(tracers, wind_x, wind_y, kdiff, rate, seg_blocks, seg_target, seg_row, seg_top):
    rows = tracers.shape[2]
    cols = tracers.shape[3]
    levels = tracers.shape[1]
    positions = rows // PR
    count = seg_target.shape[0]
    width = seg_blocks.shape[1]
    h = HALO
    row_f = seg_row.astype(jnp.float32)
    top_f = seg_top.astype(jnp.float32)
    columns = lax.axis_size("gy")
    order = jnp.arange(count, dtype=jnp.int32)
    same = seg_target[:, None] == seg_target[None, :]
    rank = jnp.sum((same & (order[:, None] < order[None, :])).astype(jnp.int32), axis=0)
    slot = seg_target * CAP + rank
    place = (slot[:, None] == jnp.arange(columns * CAP, dtype=jnp.int32)[None, :]).astype(
        jnp.float32
    )
    payload = jnp.concatenate([seg_blocks, row_f[:, None], top_f[:, None]], axis=1)
    outgoing = jnp.dot(
        place.T, payload, precision=lax.Precision.HIGHEST, preferred_element_type=jnp.float32
    )
    arrived = lax.all_to_all(
        outgoing.reshape(columns, CAP, width + 2), "gy", split_axis=0, concat_axis=0, tiled=True
    ).reshape(columns * CAP, width + 2)

    packed = jnp.concatenate(
        [
            tracers.reshape(2 * levels, rows, cols),
            wind_x,
            wind_y,
            kdiff,
            rate[None],
        ],
        axis=0,
    )
    ext = with_halo(packed, h)
    q = ext[: 2 * levels].reshape(2, levels, rows + 2 * h, cols + 2 * h)
    wx = ext[2 * levels : 3 * levels]
    wy = ext[3 * levels : 4 * levels]
    kd = ext[4 * levels : 5 * levels - 1]
    rate_ext = ext[5 * levels - 1]

    plume = plume_matrix(arrived[:, :width], arrived[:, width], arrived[:, width + 1], positions)
    injection = plume.reshape(LEV, positions, PR, cols).reshape(LEV, rows, cols)
    inj = with_halo(injection, h)

    gi = lax.axis_index("gx")
    gj = lax.axis_index("gy")
    grow = gi * rows + jnp.arange(rows + 2 * h, dtype=jnp.int32) - h
    gcol = gj * cols + jnp.arange(cols + 2 * h, dtype=jnp.int32) - h
    valid = ((grow >= 0) & (grow < lax.axis_size("gx") * rows))[:, None] & (
        (gcol >= 0) & (gcol < columns * cols)
    )[None, :]

    keep = 1.0 - jnp.exp(-rate_ext)
    factors = thomas_factor(kd)
    field = q
    for step in range(STEPS):
        advected = advect_local(field, wx, wy)
        so2 = advected[0] + inj
        loss = so2 * keep
        converted = jnp.stack([so2 - loss, advected[1] + 1.5 * loss])
        field = thomas_solve(converted, factors)
        field = jnp.where(valid, field, 0.0)
    return field[:, :, h : h + rows, h : h + cols]


def solution(mesh):
    in_specs = (
        P(None, None, "gx", "gy"),
        P(None, "gx", "gy"),
        P(None, "gx", "gy"),
        P(None, "gx", "gy"),
        P("gx", "gy"),
        P(("gx", "gy"), None),
        P(("gx", "gy")),
        P(("gx", "gy")),
        P(("gx", "gy")),
    )
    out_specs = P(None, None, "gx", "gy")
    return jax.shard_map(
        on_device, mesh=mesh, in_specs=in_specs, out_specs=out_specs, check_vma=False
    )
```

```python
import jax
import jax.numpy as jnp
from jax import lax
from jax.sharding import PartitionSpec as P

LEV = 16
STEPS = 4
PR = 16
CAP = 8
HALO = STEPS


def from_behind(value, axis, steps):
    count = lax.axis_size(axis)
    initial, last = (max(0, -steps), min(count, count - steps))
    return lax.ppermute(value, axis, [(source, source + steps) for source in range(initial, last)])


def from_corner(value, dx, dy):
    nx = lax.axis_size("gx")
    ny = lax.axis_size("gy")
    pairs = []
    for i in range(nx):
        for j in range(ny):
            ti, tj = i + dx, j + dy
            if 0 <= ti < nx and 0 <= tj < ny:
                pairs.append((i * ny + j, ti * ny + tj))
    return lax.ppermute(value, ("gx", "gy"), pairs)


def with_halo(a, h):
    c, r, w = a.shape
    top = from_behind(a[:, r - h:, :], "gx", 1)
    bottom = from_behind(a[:, :h, :], "gx", -1)
    left = from_behind(a[:, :, w - h:].reshape(c, r * h), "gy", 1).reshape(c, r, h)
    right = from_behind(a[:, :, :h].reshape(c, r * h), "gy", -1).reshape(c, r, h)
    tl = from_corner(a[:, r - h:, w - h:].reshape(c, h * h), 1, 1).reshape(c, h, h)
    tr = from_corner(a[:, r - h:, :h].reshape(c, h * h), 1, -1).reshape(c, h, h)
    bl = from_corner(a[:, :h, w - h:].reshape(c, h * h), -1, 1).reshape(c, h, h)
    br = from_corner(a[:, :h, :h].reshape(c, h * h), -1, -1).reshape(c, h, h)
    upper = jnp.concatenate([tl, top, tr], axis=2)
    middle = jnp.concatenate([left, a, right], axis=2)
    lower = jnp.concatenate([bl, bottom, br], axis=2)
    return jnp.concatenate([upper, middle, lower], axis=1)


def thomas_factor(kdiff):
    levels = kdiff.shape[0] + 1
    lower = []
    upper = []
    diag = []
    for l in range(levels):
        d_here = jnp.ones_like(kdiff[0])
        if l >= 1:
            d_here = d_here + kdiff[l - 1]
            lower.append(-kdiff[l - 1])
        else:
            lower.append(jnp.zeros_like(kdiff[0]))
        if l < levels - 1:
            d_here = d_here + kdiff[l]
            upper.append(-kdiff[l])
        else:
            upper.append(jnp.zeros_like(kdiff[0]))
        diag.append(d_here)
    inverse = []
    sweep = []
    for l in range(levels):
        if l == 0:
            denom = diag[0]
        else:
            denom = diag[l] - lower[l] * sweep[l - 1]
        inv_here = 1.0 / denom
        inverse.append(inv_here)
        sweep.append(upper[l] * inv_here)
    return (lower, inverse, sweep)


def thomas_solve(rhs, factors):
    lower, inverse, sweep = factors
    levels = len(inverse)
    forward = []
    for l in range(levels):
        if l == 0:
            forward.append(rhs[:, 0] * inverse[0])
        else:
            forward.append((rhs[:, l] - lower[l] * forward[l - 1]) * inverse[l])
    result = [None] * levels
    result[levels - 1] = forward[levels - 1]
    for l in range(levels - 2, -1, -1):
        result[l] = forward[l] - sweep[l] * result[l + 1]
    return jnp.stack(result, axis=1)


def upwind(courant, here, ahead):
    return jnp.maximum(courant, 0.0) * here + jnp.minimum(courant, 0.0) * ahead


def plume_matrix(blocks, row_f, top_f, positions):
    levels = jnp.arange(LEV, dtype=jnp.float32)
    weight = jnp.where(
        levels[None, :] < top_f[:, None], 1.0 / jnp.maximum(top_f, 1.0)[:, None], jnp.float32(0.0)
    )
    place = (row_f[:, None] == jnp.arange(positions, dtype=jnp.float32)[None, :]).astype(
        jnp.float32
    )
    mixed = (weight[:, :, None] * place[:, None, :]).reshape(blocks.shape[0], LEV * positions)
    return jnp.dot(
        mixed.T, blocks, precision=lax.Precision.HIGHEST, preferred_element_type=jnp.float32
    )


def advect_local(field, wind_x, wind_y):
    zero_row = jnp.zeros_like(field[:, :, :1, :])
    ahead_x = jnp.concatenate([field[:, :, 1:, :], zero_row], axis=2)
    flux_x = upwind(wind_x, field, ahead_x)
    before_x = jnp.concatenate([jnp.zeros_like(flux_x[:, :, :1, :]), flux_x[:, :, :-1, :]], axis=2)
    zero_col = jnp.zeros_like(field[:, :, :, :1])
    ahead_y = jnp.concatenate([field[:, :, :, 1:], zero_col], axis=3)
    flux_y = upwind(wind_y, field, ahead_y)
    before_y = jnp.concatenate([jnp.zeros_like(flux_y[:, :, :, :1]), flux_y[:, :, :, :-1]], axis=3)
    return field - (flux_x - before_x) - (flux_y - before_y)


def on_device(tracers, wind_x, wind_y, kdiff, rate, seg_blocks, seg_target, seg_row, seg_top):
    rows = tracers.shape[2]
    cols = tracers.shape[3]
    levels = tracers.shape[1]
    positions = rows // PR
    count = seg_target.shape[0]
    width = seg_blocks.shape[1]
    h = HALO
    row_f = seg_row.astype(jnp.float32)
    top_f = seg_top.astype(jnp.float32)
    columns = lax.axis_size("gy")
    order = jnp.arange(count, dtype=jnp.int32)
    same = seg_target[:, None] == seg_target[None, :]
    rank = jnp.sum((same & (order[:, None] < order[None, :])).astype(jnp.int32), axis=0)
    slot = seg_target * CAP + rank
    place = (slot[:, None] == jnp.arange(columns * CAP, dtype=jnp.int32)[None, :]).astype(
        jnp.float32
    )
    payload = jnp.concatenate([seg_blocks, row_f[:, None], top_f[:, None]], axis=1)
    outgoing = jnp.dot(
        place.T, payload, precision=lax.Precision.HIGHEST, preferred_element_type=jnp.float32
    )
    arrived = lax.all_to_all(
        outgoing.reshape(columns, CAP, width + 2), "gy", split_axis=0, concat_axis=0, tiled=True
    ).reshape(columns * CAP, width + 2)

    keep_here = 1.0 - jnp.exp(-rate)
    _, inverse_here, sweep_here = thomas_factor(kdiff)
    plume = plume_matrix(arrived[:, :width], arrived[:, width], arrived[:, width + 1], positions)
    injection = plume.reshape(LEV, positions, PR, cols).reshape(LEV, rows, cols)
    packed = jnp.concatenate(
        [
            tracers.reshape(2 * levels, rows, cols),
            wind_x,
            wind_y,
            kdiff,
            jnp.stack(inverse_here),
            jnp.stack(sweep_here[: levels - 1]),
            keep_here[None],
            injection,
        ],
        axis=0,
    )
    ext = with_halo(packed, h)
    q = ext[: 2 * levels].reshape(2, levels, rows + 2 * h, cols + 2 * h)
    at = 2 * levels
    wx = ext[at : at + levels]
    at += levels
    wy = ext[at : at + levels]
    at += levels
    kd = ext[at : at + levels - 1]
    at += levels - 1
    inverse = [ext[at + l] for l in range(levels)]
    at += levels
    sweep = [ext[at + l] for l in range(levels - 1)]
    at += levels - 1
    keep = ext[at]
    at += 1
    inj = ext[at : at + LEV]
    lower = [jnp.zeros_like(keep)] + [-kd[l] for l in range(levels - 1)]
    factors = (lower, inverse, sweep + [jnp.zeros_like(keep)])

    gi = lax.axis_index("gx")
    gj = lax.axis_index("gy")
    grow = gi * rows + jnp.arange(rows + 2 * h, dtype=jnp.int32) - h
    gcol = gj * cols + jnp.arange(cols + 2 * h, dtype=jnp.int32) - h
    valid = ((grow >= 0) & (grow < lax.axis_size("gx") * rows))[:, None] & (
        (gcol >= 0) & (gcol < columns * cols)
    )[None, :]

    field = q
    for step in range(STEPS):
        advected = advect_local(field, wx, wy)
        so2 = advected[0] + inj
        loss = so2 * keep
        converted = jnp.stack([so2 - loss, advected[1] + 1.5 * loss])
        field = thomas_solve(converted, factors)
        field = jnp.where(valid, field, 0.0)
    return field[:, :, h : h + rows, h : h + cols]


def solution(mesh):
    in_specs = (
        P(None, None, "gx", "gy"),
        P(None, "gx", "gy"),
        P(None, "gx", "gy"),
        P(None, "gx", "gy"),
        P("gx", "gy"),
        P(("gx", "gy"), None),
        P(("gx", "gy")),
        P(("gx", "gy")),
        P(("gx", "gy")),
    )
    out_specs = P(None, None, "gx", "gy")
    return jax.shard_map(
        on_device, mesh=mesh, in_specs=in_specs, out_specs=out_specs, check_vma=False
    )
```

```python
import jax
import jax.numpy as jnp
from jax import lax
from jax.sharding import PartitionSpec as P
from jax.experimental import pallas as pl
from jax.experimental.pallas import tpu as pltpu

LEV = 16
STEPS = 4
PR = 16
CAP = 8
HALO = STEPS


def from_behind(value, axis, steps):
    count = lax.axis_size(axis)
    initial, last = (max(0, -steps), min(count, count - steps))
    return lax.ppermute(value, axis, [(source, source + steps) for source in range(initial, last)])


def from_corner(value, dx, dy):
    nx = lax.axis_size("gx")
    ny = lax.axis_size("gy")
    pairs = []
    for i in range(nx):
        for j in range(ny):
            ti, tj = i + dx, j + dy
            if 0 <= ti < nx and 0 <= tj < ny:
                pairs.append((i * ny + j, ti * ny + tj))
    return lax.ppermute(value, ("gx", "gy"), pairs)


def with_halo(a, h, lanes):
    c, r, w = a.shape
    gap = jnp.zeros((c, 1, lanes - w - 2 * h), a.dtype)
    top = from_behind(a[:, r - h:, :], "gx", 1)
    bottom = from_behind(a[:, :h, :], "gx", -1)
    left = from_behind(a[:, :, w - h:].reshape(c, r * h), "gy", 1).reshape(c, r, h)
    right = from_behind(a[:, :, :h].reshape(c, r * h), "gy", -1).reshape(c, r, h)
    tl = from_corner(a[:, r - h:, w - h:].reshape(c, h * h), 1, 1).reshape(c, h, h)
    tr = from_corner(a[:, r - h:, :h].reshape(c, h * h), 1, -1).reshape(c, h, h)
    bl = from_corner(a[:, :h, w - h:].reshape(c, h * h), -1, 1).reshape(c, h, h)
    br = from_corner(a[:, :h, :h].reshape(c, h * h), -1, -1).reshape(c, h, h)

    def band(mid, after, before):
        n = mid.shape[1]
        return jnp.concatenate([mid, after, jnp.broadcast_to(gap, (c, n, gap.shape[2])), before], axis=2)

    return jnp.concatenate([band(a, right, left), band(bottom, br, bl), band(top, tr, tl)], axis=1)


def steps_kernel(ext_ref, valid_ref, o_ref, q_s, *, levels, at):
    rows_ext, lanes = valid_ref.shape
    rows, cols = o_ref.shape[2], o_ref.shape[3]
    for p in range(2 * levels):
        q_s[p] = ext_ref[p]
    valid = valid_ref[...] != 0.0
    keep = ext_ref[at["keep"]]
    zero = jnp.zeros((rows_ext, lanes), jnp.float32)

    def one_step(step, carry):
        def forward(l, prev):
            p0, p1 = prev
            wxl = ext_ref[at["wx"] + l]
            wyl = ext_ref[at["wy"] + l]

            def advect(x):
                flux_x = jnp.maximum(wxl, 0.0) * x + jnp.minimum(wxl, 0.0) * pltpu.roll(x, rows_ext - 1, 0)
                flux_y = jnp.maximum(wyl, 0.0) * x + jnp.minimum(wyl, 0.0) * pltpu.roll(x, lanes - 1, 1)
                return x - (flux_x - pltpu.roll(flux_x, 1, 0)) - (flux_y - pltpu.roll(flux_y, 1, 1))

            a0 = advect(q_s[l])
            a1 = advect(q_s[levels + l])
            so2 = a0 + ext_ref[at["inj"] + l]
            loss = so2 * keep
            c0 = so2 - loss
            c1 = a1 + 1.5 * loss
            inv = ext_ref[at["inv"] + l]
            lower = -ext_ref[at["kd"] + jnp.maximum(l - 1, 0)]
            f0 = (c0 - lower * p0) * inv
            f1 = (c1 - lower * p1) * inv
            q_s[l] = f0
            q_s[levels + l] = f1
            return (f0, f1)

        f0, f1 = lax.fori_loop(0, levels, forward, (zero, zero))
        q_s[levels - 1] = jnp.where(valid, f0, 0.0)
        q_s[2 * levels - 1] = jnp.where(valid, f1, 0.0)

        def backward(i, nxt):
            l = levels - 2 - i
            n0, n1 = nxt
            sw = ext_ref[at["sweep"] + l]
            r0 = q_s[l] - sw * n0
            r1 = q_s[levels + l] - sw * n1
            q_s[l] = jnp.where(valid, r0, 0.0)
            q_s[levels + l] = jnp.where(valid, r1, 0.0)
            return (r0, r1)

        lax.fori_loop(0, levels - 1, backward, (f0, f1))
        return carry

    lax.fori_loop(0, STEPS, one_step, 0)
    for p in range(2 * levels):
        o_ref[p // levels, p % levels] = q_s[p, 0:rows, 0:cols]


def thomas_factor(kdiff):
    levels = kdiff.shape[0] + 1
    lower = []
    upper = []
    diag = []
    for l in range(levels):
        d_here = jnp.ones_like(kdiff[0])
        if l >= 1:
            d_here = d_here + kdiff[l - 1]
            lower.append(-kdiff[l - 1])
        else:
            lower.append(jnp.zeros_like(kdiff[0]))
        if l < levels - 1:
            d_here = d_here + kdiff[l]
            upper.append(-kdiff[l])
        else:
            upper.append(jnp.zeros_like(kdiff[0]))
        diag.append(d_here)
    inverse = []
    sweep = []
    for l in range(levels):
        if l == 0:
            denom = diag[0]
        else:
            denom = diag[l] - lower[l] * sweep[l - 1]
        inv_here = 1.0 / denom
        inverse.append(inv_here)
        sweep.append(upper[l] * inv_here)
    return (lower, inverse, sweep)


def thomas_solve(rhs, factors):
    lower, inverse, sweep = factors
    levels = len(inverse)
    forward = []
    for l in range(levels):
        if l == 0:
            forward.append(rhs[:, 0] * inverse[0])
        else:
            forward.append((rhs[:, l] - lower[l] * forward[l - 1]) * inverse[l])
    result = [None] * levels
    result[levels - 1] = forward[levels - 1]
    for l in range(levels - 2, -1, -1):
        result[l] = forward[l] - sweep[l] * result[l + 1]
    return jnp.stack(result, axis=1)


def upwind(courant, here, ahead):
    return jnp.maximum(courant, 0.0) * here + jnp.minimum(courant, 0.0) * ahead


def plume_matrix(blocks, row_f, top_f, positions):
    levels = jnp.arange(LEV, dtype=jnp.float32)
    weight = jnp.where(
        levels[None, :] < top_f[:, None], 1.0 / jnp.maximum(top_f, 1.0)[:, None], jnp.float32(0.0)
    )
    place = (row_f[:, None] == jnp.arange(positions, dtype=jnp.float32)[None, :]).astype(
        jnp.float32
    )
    mixed = (weight[:, :, None] * place[:, None, :]).reshape(blocks.shape[0], LEV * positions)
    return jnp.dot(
        mixed.T, blocks, precision=lax.Precision.HIGHEST, preferred_element_type=jnp.float32
    )


def on_device(tracers, wind_x, wind_y, kdiff, rate, seg_blocks, seg_target, seg_row, seg_top):
    rows = tracers.shape[2]
    cols = tracers.shape[3]
    levels = tracers.shape[1]
    positions = rows // PR
    count = seg_target.shape[0]
    width = seg_blocks.shape[1]
    h = HALO
    row_f = seg_row.astype(jnp.float32)
    top_f = seg_top.astype(jnp.float32)
    columns = lax.axis_size("gy")
    order = jnp.arange(count, dtype=jnp.int32)
    same = seg_target[:, None] == seg_target[None, :]
    rank = jnp.sum((same & (order[:, None] < order[None, :])).astype(jnp.int32), axis=0)
    slot = seg_target * CAP + rank
    place = (slot[:, None] == jnp.arange(columns * CAP, dtype=jnp.int32)[None, :]).astype(
        jnp.float32
    )
    payload = jnp.concatenate([seg_blocks, row_f[:, None], top_f[:, None]], axis=1)
    outgoing = jnp.dot(
        place.T, payload, precision=lax.Precision.HIGHEST, preferred_element_type=jnp.float32
    )
    arrived = lax.all_to_all(
        outgoing.reshape(columns, CAP, width + 2), "gy", split_axis=0, concat_axis=0, tiled=True
    ).reshape(columns * CAP, width + 2)

    keep_here = 1.0 - jnp.exp(-rate)
    _, inverse_here, sweep_here = thomas_factor(kdiff)
    plume = plume_matrix(arrived[:, :width], arrived[:, width], arrived[:, width + 1], positions)
    injection = plume.reshape(LEV, positions, PR, cols).reshape(LEV, rows, cols)
    packed = jnp.concatenate(
        [
            tracers.reshape(2 * levels, rows, cols),
            wind_x,
            wind_y,
            kdiff,
            jnp.stack(inverse_here),
            jnp.stack(sweep_here[: levels - 1]),
            keep_here[None],
            injection,
        ],
        axis=0,
    )
    lanes = -(-(cols + 2 * h) // 128) * 128
    ext = with_halo(packed, h, lanes)
    at = {"wx": 2 * levels}
    at["wy"] = at["wx"] + levels
    at["kd"] = at["wy"] + levels
    at["inv"] = at["kd"] + levels - 1
    at["sweep"] = at["inv"] + levels
    at["keep"] = at["sweep"] + levels - 1
    at["inj"] = at["keep"] + 1

    gi = lax.axis_index("gx")
    gj = lax.axis_index("gy")
    rpos = jnp.arange(rows + 2 * h, dtype=jnp.int32)
    rpos = jnp.where(rpos < rows + h, rpos, rpos - (rows + 2 * h))
    lpos = jnp.arange(lanes, dtype=jnp.int32)
    lpos = jnp.where(lpos < cols + h, lpos, jnp.where(lpos >= lanes - h, lpos - lanes, -(cols * columns + 1)))
    grow = gi * rows + rpos
    gcol = gj * cols + lpos
    valid = (((grow >= 0) & (grow < lax.axis_size("gx") * rows))[:, None] & (
        (gcol >= 0) & (gcol < columns * cols)
    )[None, :]).astype(jnp.float32)

    kernel = lambda *refs: steps_kernel(*refs, levels=levels, at=at)
    return pl.pallas_call(
        kernel,
        out_shape=jax.ShapeDtypeStruct((2, levels, rows, cols), jnp.float32),
        scratch_shapes=[pltpu.VMEM((2 * levels, rows + 2 * h, lanes), jnp.float32)],
    )(ext, valid)


def solution(mesh):
    in_specs = (
        P(None, None, "gx", "gy"),
        P(None, "gx", "gy"),
        P(None, "gx", "gy"),
        P(None, "gx", "gy"),
        P("gx", "gy"),
        P(("gx", "gy"), None),
        P(("gx", "gy")),
        P(("gx", "gy")),
        P(("gx", "gy")),
    )
    out_specs = P(None, None, "gx", "gy")
    return jax.shard_map(
        on_device, mesh=mesh, in_specs=in_specs, out_specs=out_specs, check_vma=False
    )
```

```python
import jax
import jax.numpy as jnp
from jax import lax
from jax.sharding import PartitionSpec as P
from jax.experimental import pallas as pl
from jax.experimental.pallas import tpu as pltpu

LEV = 16
STEPS = 4
PR = 16
CAP = 8
HALO = STEPS


def from_behind(value, axis, steps):
    count = lax.axis_size(axis)
    initial, last = (max(0, -steps), min(count, count - steps))
    return lax.ppermute(value, axis, [(source, source + steps) for source in range(initial, last)])


def from_corner(value, dx, dy):
    nx = lax.axis_size("gx")
    ny = lax.axis_size("gy")
    pairs = []
    for i in range(nx):
        for j in range(ny):
            ti, tj = i + dx, j + dy
            if 0 <= ti < nx and 0 <= tj < ny:
                pairs.append((i * ny + j, ti * ny + tj))
    return lax.ppermute(value, ("gx", "gy"), pairs)


def with_halo(a, h, lanes):
    c, r, w = a.shape
    gap = jnp.zeros((c, 1, lanes - w - 2 * h), a.dtype)
    top = from_behind(a[:, r - h:, :], "gx", 1)
    bottom = from_behind(a[:, :h, :], "gx", -1)
    left = from_behind(a[:, :, w - h:].reshape(c, r * h), "gy", 1).reshape(c, r, h)
    right = from_behind(a[:, :, :h].reshape(c, r * h), "gy", -1).reshape(c, r, h)
    tl = from_corner(a[:, r - h:, w - h:].reshape(c, h * h), 1, 1).reshape(c, h, h)
    tr = from_corner(a[:, r - h:, :h].reshape(c, h * h), 1, -1).reshape(c, h, h)
    bl = from_corner(a[:, :h, w - h:].reshape(c, h * h), -1, 1).reshape(c, h, h)
    br = from_corner(a[:, :h, :h].reshape(c, h * h), -1, -1).reshape(c, h, h)

    def band(mid, after, before):
        n = mid.shape[1]
        return jnp.concatenate([mid, after, jnp.broadcast_to(gap, (c, n, gap.shape[2])), before], axis=2)

    return jnp.concatenate([band(a, right, left), band(bottom, br, bl), band(top, tr, tl)], axis=1)


def steps_kernel(ext_ref, inj_ref, valid_ref, o_ref, q_s, inv_s, sw_s, *, levels, at):
    rows_ext, lanes = valid_ref.shape
    rows, cols = o_ref.shape[2], o_ref.shape[3]
    for p in range(2 * levels):
        q_s[p] = ext_ref[p]
    valid = valid_ref[...] != 0.0
    keep = 1.0 - jnp.exp(-ext_ref[at["rate"]])
    sweep_prev = None
    for l in range(levels):
        diag = jnp.ones((rows_ext, lanes), jnp.float32)
        if l >= 1:
            diag = diag + ext_ref[at["kd"] + l - 1]
        if l < levels - 1:
            diag = diag + ext_ref[at["kd"] + l]
        if l == 0:
            denom = diag
        else:
            denom = diag - (-ext_ref[at["kd"] + l - 1]) * sweep_prev
        inv_here = 1.0 / denom
        inv_s[l] = inv_here
        if l < levels - 1:
            sweep_prev = (-ext_ref[at["kd"] + l]) * inv_here
            sw_s[l] = sweep_prev
    zero = jnp.zeros((rows_ext, lanes), jnp.float32)

    def one_step(step, carry):
        def forward(l, prev):
            p0, p1 = prev
            wxl = ext_ref[at["wx"] + l]
            wyl = ext_ref[at["wy"] + l]

            def advect(x):
                flux_x = jnp.maximum(wxl, 0.0) * x + jnp.minimum(wxl, 0.0) * pltpu.roll(x, rows_ext - 1, 0)
                flux_y = jnp.maximum(wyl, 0.0) * x + jnp.minimum(wyl, 0.0) * pltpu.roll(x, lanes - 1, 1)
                return x - (flux_x - pltpu.roll(flux_x, 1, 0)) - (flux_y - pltpu.roll(flux_y, 1, 1))

            a0 = advect(q_s[l])
            a1 = advect(q_s[levels + l])
            so2 = a0 + inj_ref[l]
            loss = so2 * keep
            c0 = so2 - loss
            c1 = a1 + 1.5 * loss
            inv = inv_s[l]
            lower = -ext_ref[at["kd"] + jnp.maximum(l - 1, 0)]
            f0 = (c0 - lower * p0) * inv
            f1 = (c1 - lower * p1) * inv
            q_s[l] = f0
            q_s[levels + l] = f1
            return (f0, f1)

        f0, f1 = lax.fori_loop(0, levels, forward, (zero, zero))
        q_s[levels - 1] = jnp.where(valid, f0, 0.0)
        q_s[2 * levels - 1] = jnp.where(valid, f1, 0.0)

        def backward(i, nxt):
            l = levels - 2 - i
            n0, n1 = nxt
            sw = sw_s[l]
            r0 = q_s[l] - sw * n0
            r1 = q_s[levels + l] - sw * n1
            q_s[l] = jnp.where(valid, r0, 0.0)
            q_s[levels + l] = jnp.where(valid, r1, 0.0)
            return (r0, r1)

        lax.fori_loop(0, levels - 1, backward, (f0, f1))
        return carry

    lax.fori_loop(0, STEPS, one_step, 0)
    for p in range(2 * levels):
        o_ref[p // levels, p % levels] = q_s[p, 0:rows, 0:cols]


def thomas_factor(kdiff):
    levels = kdiff.shape[0] + 1
    lower = []
    upper = []
    diag = []
    for l in range(levels):
        d_here = jnp.ones_like(kdiff[0])
        if l >= 1:
            d_here = d_here + kdiff[l - 1]
            lower.append(-kdiff[l - 1])
        else:
            lower.append(jnp.zeros_like(kdiff[0]))
        if l < levels - 1:
            d_here = d_here + kdiff[l]
            upper.append(-kdiff[l])
        else:
            upper.append(jnp.zeros_like(kdiff[0]))
        diag.append(d_here)
    inverse = []
    sweep = []
    for l in range(levels):
        if l == 0:
            denom = diag[0]
        else:
            denom = diag[l] - lower[l] * sweep[l - 1]
        inv_here = 1.0 / denom
        inverse.append(inv_here)
        sweep.append(upper[l] * inv_here)
    return (lower, inverse, sweep)


def thomas_solve(rhs, factors):
    lower, inverse, sweep = factors
    levels = len(inverse)
    forward = []
    for l in range(levels):
        if l == 0:
            forward.append(rhs[:, 0] * inverse[0])
        else:
            forward.append((rhs[:, l] - lower[l] * forward[l - 1]) * inverse[l])
    result = [None] * levels
    result[levels - 1] = forward[levels - 1]
    for l in range(levels - 2, -1, -1):
        result[l] = forward[l] - sweep[l] * result[l + 1]
    return jnp.stack(result, axis=1)


def upwind(courant, here, ahead):
    return jnp.maximum(courant, 0.0) * here + jnp.minimum(courant, 0.0) * ahead


def plume_matrix(blocks, row_f, top_f, positions):
    levels = jnp.arange(LEV, dtype=jnp.float32)
    weight = jnp.where(
        levels[None, :] < top_f[:, None], 1.0 / jnp.maximum(top_f, 1.0)[:, None], jnp.float32(0.0)
    )
    place = (row_f[:, None] == jnp.arange(positions, dtype=jnp.float32)[None, :]).astype(
        jnp.float32
    )
    mixed = (weight[:, :, None] * place[:, None, :]).reshape(blocks.shape[0], LEV * positions)
    return jnp.dot(
        mixed.T, blocks, precision=lax.Precision.HIGHEST, preferred_element_type=jnp.float32
    )


def on_device(tracers, wind_x, wind_y, kdiff, rate, seg_blocks, seg_target, seg_row, seg_top):
    rows = tracers.shape[2]
    cols = tracers.shape[3]
    levels = tracers.shape[1]
    positions = rows // PR
    count = seg_target.shape[0]
    width = seg_blocks.shape[1]
    h = HALO
    row_f = seg_row.astype(jnp.float32)
    top_f = seg_top.astype(jnp.float32)
    columns = lax.axis_size("gy")
    order = jnp.arange(count, dtype=jnp.int32)
    same = seg_target[:, None] == seg_target[None, :]
    rank = jnp.sum((same & (order[:, None] < order[None, :])).astype(jnp.int32), axis=0)
    slot = seg_target * CAP + rank
    place = (slot[:, None] == jnp.arange(columns * CAP, dtype=jnp.int32)[None, :]).astype(
        jnp.float32
    )
    payload = jnp.concatenate([seg_blocks, row_f[:, None], top_f[:, None]], axis=1)
    outgoing = jnp.dot(
        place.T, payload, precision=lax.Precision.HIGHEST, preferred_element_type=jnp.float32
    )
    arrived = lax.all_to_all(
        outgoing.reshape(columns, CAP, width + 2), "gy", split_axis=0, concat_axis=0, tiled=True
    ).reshape(columns * CAP, width + 2)

    lanes = -(-(cols + 2 * h) // 128) * 128
    packed = jnp.concatenate(
        [tracers.reshape(2 * levels, rows, cols), wind_x, wind_y, kdiff, rate[None]], axis=0
    )
    ext = with_halo(packed, h, lanes)
    plume = plume_matrix(arrived[:, :width], arrived[:, width], arrived[:, width + 1], positions)
    injection = plume.reshape(LEV, positions, PR, cols).reshape(LEV, rows, cols)
    inj = with_halo(injection, h, lanes)
    at = {"wx": 2 * levels}
    at["wy"] = at["wx"] + levels
    at["kd"] = at["wy"] + levels
    at["rate"] = at["kd"] + levels - 1

    gi = lax.axis_index("gx")
    gj = lax.axis_index("gy")
    rpos = jnp.arange(rows + 2 * h, dtype=jnp.int32)
    rpos = jnp.where(rpos < rows + h, rpos, rpos - (rows + 2 * h))
    lpos = jnp.arange(lanes, dtype=jnp.int32)
    lpos = jnp.where(lpos < cols + h, lpos, jnp.where(lpos >= lanes - h, lpos - lanes, -(cols * columns + 1)))
    grow = gi * rows + rpos
    gcol = gj * cols + lpos
    valid = (((grow >= 0) & (grow < lax.axis_size("gx") * rows))[:, None] & (
        (gcol >= 0) & (gcol < columns * cols)
    )[None, :]).astype(jnp.float32)

    kernel = lambda *refs: steps_kernel(*refs, levels=levels, at=at)
    return pl.pallas_call(
        kernel,
        out_shape=jax.ShapeDtypeStruct((2, levels, rows, cols), jnp.float32),
        scratch_shapes=[
            pltpu.VMEM((2 * levels, rows + 2 * h, lanes), jnp.float32),
            pltpu.VMEM((levels, rows + 2 * h, lanes), jnp.float32),
            pltpu.VMEM((levels, rows + 2 * h, lanes), jnp.float32),
        ],
    )(ext, inj, valid)


def solution(mesh):
    in_specs = (
        P(None, None, "gx", "gy"),
        P(None, "gx", "gy"),
        P(None, "gx", "gy"),
        P(None, "gx", "gy"),
        P("gx", "gy"),
        P(("gx", "gy"), None),
        P(("gx", "gy")),
        P(("gx", "gy")),
        P(("gx", "gy")),
    )
    out_specs = P(None, None, "gx", "gy")
    return jax.shard_map(
        on_device, mesh=mesh, in_specs=in_specs, out_specs=out_specs, check_vma=False
    )
```

```python
import jax
import jax.numpy as jnp
from jax import lax
from jax.sharding import PartitionSpec as P
from jax.experimental import pallas as pl
from jax.experimental.pallas import tpu as pltpu

LEV = 16
STEPS = 4
PR = 16
CAP = 8
HALO = STEPS


def from_behind(value, axis, steps):
    count = lax.axis_size(axis)
    initial, last = (max(0, -steps), min(count, count - steps))
    return lax.ppermute(value, axis, [(source, source + steps) for source in range(initial, last)])


def from_corner(value, dx, dy):
    nx = lax.axis_size("gx")
    ny = lax.axis_size("gy")
    pairs = []
    for i in range(nx):
        for j in range(ny):
            ti, tj = i + dx, j + dy
            if 0 <= ti < nx and 0 <= tj < ny:
                pairs.append((i * ny + j, ti * ny + tj))
    return lax.ppermute(value, ("gx", "gy"), pairs)


def with_halo(a, h, lanes):
    c, r, w = a.shape
    gap = jnp.zeros((c, 1, lanes - w - 2 * h), a.dtype)
    top = from_behind(a[:, r - h:, :], "gx", 1)
    bottom = from_behind(a[:, :h, :], "gx", -1)
    left = from_behind(a[:, :, w - h:].reshape(c, r * h), "gy", 1).reshape(c, r, h)
    right = from_behind(a[:, :, :h].reshape(c, r * h), "gy", -1).reshape(c, r, h)
    tl = from_corner(a[:, r - h:, w - h:].reshape(c, h * h), 1, 1).reshape(c, h, h)
    tr = from_corner(a[:, r - h:, :h].reshape(c, h * h), 1, -1).reshape(c, h, h)
    bl = from_corner(a[:, :h, w - h:].reshape(c, h * h), -1, 1).reshape(c, h, h)
    br = from_corner(a[:, :h, :h].reshape(c, h * h), -1, -1).reshape(c, h, h)

    def band(mid, after, before):
        n = mid.shape[1]
        return jnp.concatenate([mid, after, jnp.broadcast_to(gap, (c, n, gap.shape[2])), before], axis=2)

    return jnp.concatenate([band(a, right, left), band(bottom, br, bl), band(top, tr, tl)], axis=1)


def steps_kernel(ext_ref, inj_ref, valid_ref, o_ref, q_s, inv_s, sw_s, *, levels, at):
    rows_ext, lanes = valid_ref.shape
    rows, cols = o_ref.shape[2], o_ref.shape[3]
    for p in range(2 * levels):
        q_s[p] = ext_ref[p]
    valid = valid_ref[...] != 0.0
    keep = 1.0 - jnp.exp(-ext_ref[at["rate"]])
    sweep_prev = None
    for l in range(levels):
        diag = jnp.ones((rows_ext, lanes), jnp.float32)
        if l >= 1:
            diag = diag + ext_ref[at["kd"] + l - 1]
        if l < levels - 1:
            diag = diag + ext_ref[at["kd"] + l]
        if l == 0:
            denom = diag
        else:
            denom = diag - (-ext_ref[at["kd"] + l - 1]) * sweep_prev
        inv_here = 1.0 / denom
        inv_s[l] = inv_here
        if l < levels - 1:
            sweep_prev = (-ext_ref[at["kd"] + l]) * inv_here
            sw_s[l] = sweep_prev
    zero = jnp.zeros((rows_ext, lanes), jnp.float32)

    def one_step(step, carry):
        def forward(l, prev):
            p0, p1 = prev
            wxl = ext_ref[at["wx"] + l]
            wyl = ext_ref[at["wy"] + l]

            def advect(x):
                flux_x = jnp.maximum(wxl, 0.0) * x + jnp.minimum(wxl, 0.0) * pltpu.roll(x, rows_ext - 1, 0)
                flux_y = jnp.maximum(wyl, 0.0) * x + jnp.minimum(wyl, 0.0) * pltpu.roll(x, lanes - 1, 1)
                return x - (flux_x - pltpu.roll(flux_x, 1, 0)) - (flux_y - pltpu.roll(flux_y, 1, 1))

            a0 = advect(q_s[l])
            a1 = advect(q_s[levels + l])
            so2 = a0 + inj_ref[l]
            loss = so2 * keep
            c0 = so2 - loss
            c1 = a1 + 1.5 * loss
            inv = inv_s[l]
            lower = -ext_ref[at["kd"] + jnp.maximum(l - 1, 0)]
            f0 = (c0 - lower * p0) * inv
            f1 = (c1 - lower * p1) * inv
            q_s[l] = f0
            q_s[levels + l] = f1
            return (f0, f1)

        f0, f1 = lax.fori_loop(0, levels, forward, (zero, zero))
        q_s[levels - 1] = jnp.where(valid, f0, 0.0)
        q_s[2 * levels - 1] = jnp.where(valid, f1, 0.0)

        def backward(i, nxt):
            l = levels - 2 - i
            n0, n1 = nxt
            sw = sw_s[l]
            r0 = q_s[l] - sw * n0
            r1 = q_s[levels + l] - sw * n1
            q_s[l] = jnp.where(valid, r0, 0.0)
            q_s[levels + l] = jnp.where(valid, r1, 0.0)
            return (r0, r1)

        lax.fori_loop(0, levels - 1, backward, (f0, f1))
        return carry

    lax.fori_loop(0, STEPS, one_step, 0)
    for p in range(2 * levels):
        o_ref[p // levels, p % levels] = q_s[p, 0:rows, 0:cols]


def thomas_factor(kdiff):
    levels = kdiff.shape[0] + 1
    lower = []
    upper = []
    diag = []
    for l in range(levels):
        d_here = jnp.ones_like(kdiff[0])
        if l >= 1:
            d_here = d_here + kdiff[l - 1]
            lower.append(-kdiff[l - 1])
        else:
            lower.append(jnp.zeros_like(kdiff[0]))
        if l < levels - 1:
            d_here = d_here + kdiff[l]
            upper.append(-kdiff[l])
        else:
            upper.append(jnp.zeros_like(kdiff[0]))
        diag.append(d_here)
    inverse = []
    sweep = []
    for l in range(levels):
        if l == 0:
            denom = diag[0]
        else:
            denom = diag[l] - lower[l] * sweep[l - 1]
        inv_here = 1.0 / denom
        inverse.append(inv_here)
        sweep.append(upper[l] * inv_here)
    return (lower, inverse, sweep)


def thomas_solve(rhs, factors):
    lower, inverse, sweep = factors
    levels = len(inverse)
    forward = []
    for l in range(levels):
        if l == 0:
            forward.append(rhs[:, 0] * inverse[0])
        else:
            forward.append((rhs[:, l] - lower[l] * forward[l - 1]) * inverse[l])
    result = [None] * levels
    result[levels - 1] = forward[levels - 1]
    for l in range(levels - 2, -1, -1):
        result[l] = forward[l] - sweep[l] * result[l + 1]
    return jnp.stack(result, axis=1)


def upwind(courant, here, ahead):
    return jnp.maximum(courant, 0.0) * here + jnp.minimum(courant, 0.0) * ahead


def plume_matrix(blocks, row_f, top_f, positions):
    levels = jnp.arange(LEV, dtype=jnp.float32)
    weight = jnp.where(
        levels[None, :] < top_f[:, None], 1.0 / jnp.maximum(top_f, 1.0)[:, None], jnp.float32(0.0)
    )
    place = (row_f[:, None] == jnp.arange(positions, dtype=jnp.float32)[None, :]).astype(
        jnp.float32
    )
    mixed = (weight[:, :, None] * place[:, None, :]).reshape(blocks.shape[0], LEV * positions)
    return jnp.dot(
        mixed.T, blocks, precision=lax.Precision.HIGHEST, preferred_element_type=jnp.float32
    )


def on_device(tracers, wind_x, wind_y, kdiff, rate, seg_blocks, seg_target, seg_row, seg_top):
    rows = tracers.shape[2]
    cols = tracers.shape[3]
    levels = tracers.shape[1]
    positions = rows // PR
    count = seg_target.shape[0]
    width = seg_blocks.shape[1]
    h = HALO
    row_f = seg_row.astype(jnp.float32)
    top_f = seg_top.astype(jnp.float32)
    columns = lax.axis_size("gy")
    order = jnp.arange(count, dtype=jnp.int32)
    same = seg_target[:, None] == seg_target[None, :]
    rank = jnp.sum((same & (order[:, None] < order[None, :])).astype(jnp.int32), axis=0)
    slot = seg_target * CAP + rank
    place = (slot[:, None] == jnp.arange(columns * CAP, dtype=jnp.int32)[None, :]).astype(
        jnp.float32
    )
    payload = jnp.concatenate([seg_blocks, row_f[:, None], top_f[:, None]], axis=1)
    outgoing = jnp.dot(
        place.T, payload, precision=lax.Precision.HIGHEST, preferred_element_type=jnp.float32
    )
    main = outgoing.reshape(columns, CAP, width + 2)
    details = main[:, :, width:]
    shaped = main[:, :, :width].reshape(columns, CAP, PR, cols)
    tail_cols = jnp.concatenate([shaped[:, :, :, cols - h:].reshape(columns, CAP, PR * h), details], axis=2)
    head_cols = jnp.concatenate([shaped[:, :, :, :h].reshape(columns, CAP, PR * h), details], axis=2)
    empty = jnp.zeros_like(tail_cols[:1])
    to_left_halo = jnp.concatenate([empty, tail_cols[:-1]], axis=0)
    to_right_halo = jnp.concatenate([head_cols[1:], empty], axis=0)
    edge = PR * h + 2
    arrived = lax.all_to_all(
        jnp.concatenate([main, to_left_halo, to_right_halo], axis=2),
        "gy",
        split_axis=0,
        concat_axis=0,
        tiled=True,
    ).reshape(columns * CAP, width + 2 + 2 * edge)

    lanes = -(-(cols + 2 * h) // 128) * 128
    packed = jnp.concatenate(
        [tracers.reshape(2 * levels, rows, cols), wind_x, wind_y, kdiff, rate[None]], axis=0
    )
    ext = with_halo(packed, h, lanes)

    def injected(part, span):
        plume = plume_matrix(part[:, : PR * span], part[:, PR * span], part[:, PR * span + 1], positions)
        return plume.reshape(LEV, positions, PR, span).reshape(LEV, rows, span)

    injection = injected(arrived[:, : width + 2], cols)
    left = injected(arrived[:, width + 2 : width + 2 + edge], h)
    right = injected(arrived[:, width + 2 + edge :], h)
    gap = jnp.zeros((LEV, rows, lanes - cols - 2 * h), jnp.float32)
    band = jnp.concatenate([injection, right, gap, left], axis=2)
    below = from_behind(band[:, :h], "gx", -1)
    above = from_behind(band[:, rows - h :], "gx", 1)
    inj = jnp.concatenate([band, below, above], axis=1)
    at = {"wx": 2 * levels}
    at["wy"] = at["wx"] + levels
    at["kd"] = at["wy"] + levels
    at["rate"] = at["kd"] + levels - 1

    gi = lax.axis_index("gx")
    gj = lax.axis_index("gy")
    rpos = jnp.arange(rows + 2 * h, dtype=jnp.int32)
    rpos = jnp.where(rpos < rows + h, rpos, rpos - (rows + 2 * h))
    lpos = jnp.arange(lanes, dtype=jnp.int32)
    lpos = jnp.where(lpos < cols + h, lpos, jnp.where(lpos >= lanes - h, lpos - lanes, -(cols * columns + 1)))
    grow = gi * rows + rpos
    gcol = gj * cols + lpos
    valid = (((grow >= 0) & (grow < lax.axis_size("gx") * rows))[:, None] & (
        (gcol >= 0) & (gcol < columns * cols)
    )[None, :]).astype(jnp.float32)

    kernel = lambda *refs: steps_kernel(*refs, levels=levels, at=at)
    return pl.pallas_call(
        kernel,
        out_shape=jax.ShapeDtypeStruct((2, levels, rows, cols), jnp.float32),
        scratch_shapes=[
            pltpu.VMEM((2 * levels, rows + 2 * h, lanes), jnp.float32),
            pltpu.VMEM((levels, rows + 2 * h, lanes), jnp.float32),
            pltpu.VMEM((levels, rows + 2 * h, lanes), jnp.float32),
        ],
    )(ext, inj, valid)


def solution(mesh):
    in_specs = (
        P(None, None, "gx", "gy"),
        P(None, "gx", "gy"),
        P(None, "gx", "gy"),
        P(None, "gx", "gy"),
        P("gx", "gy"),
        P(("gx", "gy"), None),
        P(("gx", "gy")),
        P(("gx", "gy")),
        P(("gx", "gy")),
    )
    out_specs = P(None, None, "gx", "gy")
    return jax.shard_map(
        on_device, mesh=mesh, in_specs=in_specs, out_specs=out_specs, check_vma=False
    )
```

```python
import jax
import jax.numpy as jnp
from jax import lax
from jax.sharding import PartitionSpec as P
from jax.experimental import pallas as pl
from jax.experimental.pallas import tpu as pltpu

LEV = 16
STEPS = 4
PR = 16
CAP = 8
HALO = STEPS


def from_behind(value, axis, steps):
    count = lax.axis_size(axis)
    initial, last = (max(0, -steps), min(count, count - steps))
    return lax.ppermute(value, axis, [(source, source + steps) for source in range(initial, last)])


def rows_halo(band, h):
    r = band.shape[1]
    below = from_behind(band[:, :h], "gx", -1)
    above = from_behind(band[:, r - h :], "gx", 1)
    return jnp.concatenate([band, below, above], axis=1)


def with_halo(a, h, lanes):
    c, r, w = a.shape
    gap = jnp.zeros((c, r, lanes - w - 2 * h), a.dtype)
    left = from_behind(a[:, :, w - h:].reshape(c, r * h), "gy", 1).reshape(c, r, h)
    right = from_behind(a[:, :, :h].reshape(c, r * h), "gy", -1).reshape(c, r, h)
    return rows_halo(jnp.concatenate([a, right, gap, left], axis=2), h)


def steps_kernel(ext_ref, inj_ref, valid_ref, o_ref, q_s, inv_s, sw_s, *, levels, at):
    rows_ext, lanes = valid_ref.shape
    rows, cols = o_ref.shape[2], o_ref.shape[3]
    for p in range(2 * levels):
        q_s[p] = ext_ref[p]
    valid = valid_ref[...] != 0.0
    keep = 1.0 - jnp.exp(-ext_ref[at["rate"]])
    sweep_prev = None
    for l in range(levels):
        diag = jnp.ones((rows_ext, lanes), jnp.float32)
        if l >= 1:
            diag = diag + ext_ref[at["kd"] + l - 1]
        if l < levels - 1:
            diag = diag + ext_ref[at["kd"] + l]
        if l == 0:
            denom = diag
        else:
            denom = diag - (-ext_ref[at["kd"] + l - 1]) * sweep_prev
        inv_here = 1.0 / denom
        inv_s[l] = inv_here
        if l < levels - 1:
            sweep_prev = (-ext_ref[at["kd"] + l]) * inv_here
            sw_s[l] = sweep_prev
    zero = jnp.zeros((rows_ext, lanes), jnp.float32)

    def one_step(step, carry):
        def forward(l, prev):
            p0, p1 = prev
            wxl = ext_ref[at["wx"] + l]
            wyl = ext_ref[at["wy"] + l]

            def advect(x):
                flux_x = jnp.maximum(wxl, 0.0) * x + jnp.minimum(wxl, 0.0) * pltpu.roll(x, rows_ext - 1, 0)
                flux_y = jnp.maximum(wyl, 0.0) * x + jnp.minimum(wyl, 0.0) * pltpu.roll(x, lanes - 1, 1)
                return x - (flux_x - pltpu.roll(flux_x, 1, 0)) - (flux_y - pltpu.roll(flux_y, 1, 1))

            a0 = advect(q_s[l])
            a1 = advect(q_s[levels + l])
            so2 = a0 + inj_ref[l]
            loss = so2 * keep
            c0 = so2 - loss
            c1 = a1 + 1.5 * loss
            inv = inv_s[l]
            lower = -ext_ref[at["kd"] + jnp.maximum(l - 1, 0)]
            f0 = (c0 - lower * p0) * inv
            f1 = (c1 - lower * p1) * inv
            q_s[l] = f0
            q_s[levels + l] = f1
            return (f0, f1)

        f0, f1 = lax.fori_loop(0, levels, forward, (zero, zero))
        q_s[levels - 1] = jnp.where(valid, f0, 0.0)
        q_s[2 * levels - 1] = jnp.where(valid, f1, 0.0)

        def backward(i, nxt):
            l = levels - 2 - i
            n0, n1 = nxt
            sw = sw_s[l]
            r0 = q_s[l] - sw * n0
            r1 = q_s[levels + l] - sw * n1
            q_s[l] = jnp.where(valid, r0, 0.0)
            q_s[levels + l] = jnp.where(valid, r1, 0.0)
            return (r0, r1)

        lax.fori_loop(0, levels - 1, backward, (f0, f1))
        return carry

    lax.fori_loop(0, STEPS, one_step, 0)
    for p in range(2 * levels):
        o_ref[p // levels, p % levels] = q_s[p, 0:rows, 0:cols]


def thomas_factor(kdiff):
    levels = kdiff.shape[0] + 1
    lower = []
    upper = []
    diag = []
    for l in range(levels):
        d_here = jnp.ones_like(kdiff[0])
        if l >= 1:
            d_here = d_here + kdiff[l - 1]
            lower.append(-kdiff[l - 1])
        else:
            lower.append(jnp.zeros_like(kdiff[0]))
        if l < levels - 1:
            d_here = d_here + kdiff[l]
            upper.append(-kdiff[l])
        else:
            upper.append(jnp.zeros_like(kdiff[0]))
        diag.append(d_here)
    inverse = []
    sweep = []
    for l in range(levels):
        if l == 0:
            denom = diag[0]
        else:
            denom = diag[l] - lower[l] * sweep[l - 1]
        inv_here = 1.0 / denom
        inverse.append(inv_here)
        sweep.append(upper[l] * inv_here)
    return (lower, inverse, sweep)


def thomas_solve(rhs, factors):
    lower, inverse, sweep = factors
    levels = len(inverse)
    forward = []
    for l in range(levels):
        if l == 0:
            forward.append(rhs[:, 0] * inverse[0])
        else:
            forward.append((rhs[:, l] - lower[l] * forward[l - 1]) * inverse[l])
    result = [None] * levels
    result[levels - 1] = forward[levels - 1]
    for l in range(levels - 2, -1, -1):
        result[l] = forward[l] - sweep[l] * result[l + 1]
    return jnp.stack(result, axis=1)


def upwind(courant, here, ahead):
    return jnp.maximum(courant, 0.0) * here + jnp.minimum(courant, 0.0) * ahead


def plume_matrix(blocks, row_f, top_f, positions):
    levels = jnp.arange(LEV, dtype=jnp.float32)
    weight = jnp.where(
        levels[None, :] < top_f[:, None], 1.0 / jnp.maximum(top_f, 1.0)[:, None], jnp.float32(0.0)
    )
    place = (row_f[:, None] == jnp.arange(positions, dtype=jnp.float32)[None, :]).astype(
        jnp.float32
    )
    mixed = (weight[:, :, None] * place[:, None, :]).reshape(blocks.shape[0], LEV * positions)
    return jnp.dot(
        mixed.T, blocks, precision=lax.Precision.HIGHEST, preferred_element_type=jnp.float32
    )


def on_device(tracers, wind_x, wind_y, kdiff, rate, seg_blocks, seg_target, seg_row, seg_top):
    rows = tracers.shape[2]
    cols = tracers.shape[3]
    levels = tracers.shape[1]
    positions = rows // PR
    count = seg_target.shape[0]
    width = seg_blocks.shape[1]
    h = HALO
    row_f = seg_row.astype(jnp.float32)
    top_f = seg_top.astype(jnp.float32)
    columns = lax.axis_size("gy")
    order = jnp.arange(count, dtype=jnp.int32)
    same = seg_target[:, None] == seg_target[None, :]
    rank = jnp.sum((same & (order[:, None] < order[None, :])).astype(jnp.int32), axis=0)
    slot = seg_target * CAP + rank
    place = (slot[:, None] == jnp.arange(columns * CAP, dtype=jnp.int32)[None, :]).astype(
        jnp.float32
    )
    payload = jnp.concatenate([seg_blocks, row_f[:, None], top_f[:, None]], axis=1)
    outgoing = jnp.dot(
        place.T, payload, precision=lax.Precision.HIGHEST, preferred_element_type=jnp.float32
    )
    main = outgoing.reshape(columns, CAP, width + 2)
    details = main[:, :, width:]
    shaped = main[:, :, :width].reshape(columns, CAP, PR, cols)
    tail_cols = jnp.concatenate([shaped[:, :, :, cols - h:].reshape(columns, CAP, PR * h), details], axis=2)
    head_cols = jnp.concatenate([shaped[:, :, :, :h].reshape(columns, CAP, PR * h), details], axis=2)
    empty = jnp.zeros_like(tail_cols[:1])
    to_left_halo = jnp.concatenate([empty, tail_cols[:-1]], axis=0)
    to_right_halo = jnp.concatenate([head_cols[1:], empty], axis=0)
    edge = PR * h + 2
    arrived = lax.all_to_all(
        jnp.concatenate([main, to_left_halo, to_right_halo], axis=2),
        "gy",
        split_axis=0,
        concat_axis=0,
        tiled=True,
    ).reshape(columns * CAP, width + 2 + 2 * edge)

    lanes = -(-(cols + 2 * h) // 128) * 128
    packed = jnp.concatenate(
        [tracers.reshape(2 * levels, rows, cols), wind_x, wind_y, kdiff, rate[None]], axis=0
    )
    ext = with_halo(packed, h, lanes)

    def injected(part, span):
        plume = plume_matrix(part[:, : PR * span], part[:, PR * span], part[:, PR * span + 1], positions)
        return plume.reshape(LEV, positions, PR, span).reshape(LEV, rows, span)

    injection = injected(arrived[:, : width + 2], cols)
    left = injected(arrived[:, width + 2 : width + 2 + edge], h)
    right = injected(arrived[:, width + 2 + edge :], h)
    gap = jnp.zeros((LEV, rows, lanes - cols - 2 * h), jnp.float32)
    band = jnp.concatenate([injection, right, gap, left], axis=2)
    inj = rows_halo(band, h)
    at = {"wx": 2 * levels}
    at["wy"] = at["wx"] + levels
    at["kd"] = at["wy"] + levels
    at["rate"] = at["kd"] + levels - 1

    gi = lax.axis_index("gx")
    gj = lax.axis_index("gy")
    rpos = jnp.arange(rows + 2 * h, dtype=jnp.int32)
    rpos = jnp.where(rpos < rows + h, rpos, rpos - (rows + 2 * h))
    lpos = jnp.arange(lanes, dtype=jnp.int32)
    lpos = jnp.where(lpos < cols + h, lpos, jnp.where(lpos >= lanes - h, lpos - lanes, -(cols * columns + 1)))
    grow = gi * rows + rpos
    gcol = gj * cols + lpos
    valid = (((grow >= 0) & (grow < lax.axis_size("gx") * rows))[:, None] & (
        (gcol >= 0) & (gcol < columns * cols)
    )[None, :]).astype(jnp.float32)

    kernel = lambda *refs: steps_kernel(*refs, levels=levels, at=at)
    return pl.pallas_call(
        kernel,
        out_shape=jax.ShapeDtypeStruct((2, levels, rows, cols), jnp.float32),
        scratch_shapes=[
            pltpu.VMEM((2 * levels, rows + 2 * h, lanes), jnp.float32),
            pltpu.VMEM((levels, rows + 2 * h, lanes), jnp.float32),
            pltpu.VMEM((levels, rows + 2 * h, lanes), jnp.float32),
        ],
    )(ext, inj, valid)


def solution(mesh):
    in_specs = (
        P(None, None, "gx", "gy"),
        P(None, "gx", "gy"),
        P(None, "gx", "gy"),
        P(None, "gx", "gy"),
        P("gx", "gy"),
        P(("gx", "gy"), None),
        P(("gx", "gy")),
        P(("gx", "gy")),
        P(("gx", "gy")),
    )
    out_specs = P(None, None, "gx", "gy")
    return jax.shard_map(
        on_device, mesh=mesh, in_specs=in_specs, out_specs=out_specs, check_vma=False
    )
```

```python
import jax
import jax.numpy as jnp
from jax import lax
from jax.sharding import PartitionSpec as P
from jax.experimental import pallas as pl
from jax.experimental.pallas import tpu as pltpu

LEV = 16
STEPS = 4
PR = 16
CAP = 8
HALO = STEPS


def from_behind(value, axis, steps):
    count = lax.axis_size(axis)
    initial, last = (max(0, -steps), min(count, count - steps))
    return lax.ppermute(value, axis, [(source, source + steps) for source in range(initial, last)])


def rows_halo(band, h):
    r = band.shape[1]
    below = from_behind(band[:, :h], "gx", -1)
    above = from_behind(band[:, r - h :], "gx", 1)
    return jnp.concatenate([band, below, above], axis=1)


def column_halo(a, h):
    c, r, w = a.shape
    left = from_behind(a[:, :, w - h:].reshape(c, r * h), "gy", 1).reshape(c, r, h)
    right = from_behind(a[:, :, :h].reshape(c, r * h), "gy", -1).reshape(c, r, h)
    return left, right


def with_halo(a, left, right, h, lanes):
    c, r, w = a.shape
    gap = jnp.zeros((c, r, lanes - w - 2 * h), a.dtype)
    return rows_halo(jnp.concatenate([a, right, gap, left], axis=2), h)


def steps_kernel(ext_ref, inj_ref, valid_ref, o_ref, q_s, inv_s, sw_s, *, levels, at):
    rows_ext, lanes = valid_ref.shape
    rows, cols = o_ref.shape[2], o_ref.shape[3]
    for p in range(2 * levels):
        q_s[p] = ext_ref[p]
    valid = valid_ref[...] != 0.0
    keep = 1.0 - jnp.exp(-ext_ref[at["rate"]])
    sweep_prev = None
    for l in range(levels):
        diag = jnp.ones((rows_ext, lanes), jnp.float32)
        if l >= 1:
            diag = diag + ext_ref[at["kd"] + l - 1]
        if l < levels - 1:
            diag = diag + ext_ref[at["kd"] + l]
        if l == 0:
            denom = diag
        else:
            denom = diag - (-ext_ref[at["kd"] + l - 1]) * sweep_prev
        inv_here = 1.0 / denom
        inv_s[l] = inv_here
        if l < levels - 1:
            sweep_prev = (-ext_ref[at["kd"] + l]) * inv_here
            sw_s[l] = sweep_prev
    zero = jnp.zeros((rows_ext, lanes), jnp.float32)

    def one_step(step, carry):
        def forward(l, prev):
            p0, p1 = prev
            wxl = ext_ref[at["wx"] + l]
            wyl = ext_ref[at["wy"] + l]
            out_x = jnp.maximum(wxl, 0.0)
            in_x = jnp.minimum(wxl, 0.0)
            out_y = jnp.maximum(wyl, 0.0)
            in_y = jnp.minimum(wyl, 0.0)

            def advect(x):
                flux_x = out_x * x + in_x * pltpu.roll(x, rows_ext - 1, 0)
                flux_y = out_y * x + in_y * pltpu.roll(x, lanes - 1, 1)
                return x - (flux_x - pltpu.roll(flux_x, 1, 0)) - (flux_y - pltpu.roll(flux_y, 1, 1))

            a0 = advect(q_s[l])
            a1 = advect(q_s[levels + l])
            so2 = a0 + inj_ref[l]
            loss = so2 * keep
            c0 = so2 - loss
            c1 = a1 + 1.5 * loss
            inv = inv_s[l]
            lower = -ext_ref[at["kd"] + jnp.maximum(l - 1, 0)]
            f0 = (c0 - lower * p0) * inv
            f1 = (c1 - lower * p1) * inv
            q_s[l] = f0
            q_s[levels + l] = f1
            return (f0, f1)

        f0, f1 = lax.fori_loop(0, levels, forward, (zero, zero))
        q_s[levels - 1] = jnp.where(valid, f0, 0.0)
        q_s[2 * levels - 1] = jnp.where(valid, f1, 0.0)

        def backward(i, nxt):
            l = levels - 2 - i
            n0, n1 = nxt
            sw = sw_s[l]
            r0 = q_s[l] - sw * n0
            r1 = q_s[levels + l] - sw * n1
            q_s[l] = jnp.where(valid, r0, 0.0)
            q_s[levels + l] = jnp.where(valid, r1, 0.0)
            return (r0, r1)

        lax.fori_loop(0, levels - 1, backward, (f0, f1))
        return carry

    lax.fori_loop(0, STEPS, one_step, 0)
    for p in range(2 * levels):
        o_ref[p // levels, p % levels] = q_s[p, 0:rows, 0:cols]


def thomas_factor(kdiff):
    levels = kdiff.shape[0] + 1
    lower = []
    upper = []
    diag = []
    for l in range(levels):
        d_here = jnp.ones_like(kdiff[0])
        if l >= 1:
            d_here = d_here + kdiff[l - 1]
            lower.append(-kdiff[l - 1])
        else:
            lower.append(jnp.zeros_like(kdiff[0]))
        if l < levels - 1:
            d_here = d_here + kdiff[l]
            upper.append(-kdiff[l])
        else:
            upper.append(jnp.zeros_like(kdiff[0]))
        diag.append(d_here)
    inverse = []
    sweep = []
    for l in range(levels):
        if l == 0:
            denom = diag[0]
        else:
            denom = diag[l] - lower[l] * sweep[l - 1]
        inv_here = 1.0 / denom
        inverse.append(inv_here)
        sweep.append(upper[l] * inv_here)
    return (lower, inverse, sweep)


def thomas_solve(rhs, factors):
    lower, inverse, sweep = factors
    levels = len(inverse)
    forward = []
    for l in range(levels):
        if l == 0:
            forward.append(rhs[:, 0] * inverse[0])
        else:
            forward.append((rhs[:, l] - lower[l] * forward[l - 1]) * inverse[l])
    result = [None] * levels
    result[levels - 1] = forward[levels - 1]
    for l in range(levels - 2, -1, -1):
        result[l] = forward[l] - sweep[l] * result[l + 1]
    return jnp.stack(result, axis=1)


def upwind(courant, here, ahead):
    return jnp.maximum(courant, 0.0) * here + jnp.minimum(courant, 0.0) * ahead


def plume_matrix(blocks, row_f, top_f, positions):
    levels = jnp.arange(LEV, dtype=jnp.float32)
    weight = jnp.where(
        levels[None, :] < top_f[:, None], 1.0 / jnp.maximum(top_f, 1.0)[:, None], jnp.float32(0.0)
    )
    place = (row_f[:, None] == jnp.arange(positions, dtype=jnp.float32)[None, :]).astype(
        jnp.float32
    )
    mixed = (weight[:, :, None] * place[:, None, :]).reshape(blocks.shape[0], LEV * positions)
    return jnp.dot(
        mixed.T, blocks, precision=lax.Precision.HIGHEST, preferred_element_type=jnp.float32
    )


def on_device(tracers, wind_x, wind_y, kdiff, rate, seg_blocks, seg_target, seg_row, seg_top):
    rows = tracers.shape[2]
    cols = tracers.shape[3]
    levels = tracers.shape[1]
    positions = rows // PR
    count = seg_target.shape[0]
    width = seg_blocks.shape[1]
    h = HALO
    row_f = seg_row.astype(jnp.float32)
    top_f = seg_top.astype(jnp.float32)
    columns = lax.axis_size("gy")
    order = jnp.arange(count, dtype=jnp.int32)
    same = seg_target[:, None] == seg_target[None, :]
    rank = jnp.sum((same & (order[:, None] < order[None, :])).astype(jnp.int32), axis=0)
    slot = seg_target * CAP + rank
    place = (slot[:, None] == jnp.arange(columns * CAP, dtype=jnp.int32)[None, :]).astype(
        jnp.float32
    )
    payload = jnp.concatenate([seg_blocks, row_f[:, None], top_f[:, None]], axis=1)
    outgoing = jnp.dot(
        place.T, payload, precision=lax.Precision.HIGHEST, preferred_element_type=jnp.float32
    )
    main = outgoing.reshape(columns, CAP, width + 2)
    details = main[:, :, width:]
    shaped = main[:, :, :width].reshape(columns, CAP, PR, cols)
    tail_cols = jnp.concatenate([shaped[:, :, :, cols - h:].reshape(columns, CAP, PR * h), details], axis=2)
    head_cols = jnp.concatenate([shaped[:, :, :, :h].reshape(columns, CAP, PR * h), details], axis=2)
    empty = jnp.zeros_like(tail_cols[:1])
    to_left_halo = jnp.concatenate([empty, tail_cols[:-1]], axis=0)
    to_right_halo = jnp.concatenate([head_cols[1:], empty], axis=0)
    edge = PR * h + 2
    lanes = -(-(cols + 2 * h) // 128) * 128
    packed = jnp.concatenate(
        [tracers.reshape(2 * levels, rows, cols), wind_x, wind_y, kdiff, rate[None]], axis=0
    )
    left_cols, right_cols = column_halo(packed, h)
    sendable, left_cols, right_cols = lax.optimization_barrier(
        (jnp.concatenate([main, to_left_halo, to_right_halo], axis=2), left_cols, right_cols)
    )
    arrived = lax.all_to_all(
        sendable,
        "gy",
        split_axis=0,
        concat_axis=0,
        tiled=True,
    ).reshape(columns * CAP, width + 2 + 2 * edge)

    ext = with_halo(packed, left_cols, right_cols, h, lanes)

    def injected(part, span):
        plume = plume_matrix(part[:, : PR * span], part[:, PR * span], part[:, PR * span + 1], positions)
        return plume.reshape(LEV, positions, PR, span).reshape(LEV, rows, span)

    injection = injected(arrived[:, : width + 2], cols)
    left = injected(arrived[:, width + 2 : width + 2 + edge], h)
    right = injected(arrived[:, width + 2 + edge :], h)
    gap = jnp.zeros((LEV, rows, lanes - cols - 2 * h), jnp.float32)
    band = jnp.concatenate([injection, right, gap, left], axis=2)
    inj = rows_halo(band, h)
    at = {"wx": 2 * levels}
    at["wy"] = at["wx"] + levels
    at["kd"] = at["wy"] + levels
    at["rate"] = at["kd"] + levels - 1

    gi = lax.axis_index("gx")
    gj = lax.axis_index("gy")
    rpos = jnp.arange(rows + 2 * h, dtype=jnp.int32)
    rpos = jnp.where(rpos < rows + h, rpos, rpos - (rows + 2 * h))
    lpos = jnp.arange(lanes, dtype=jnp.int32)
    lpos = jnp.where(lpos < cols + h, lpos, jnp.where(lpos >= lanes - h, lpos - lanes, -(cols * columns + 1)))
    grow = gi * rows + rpos
    gcol = gj * cols + lpos
    valid = (((grow >= 0) & (grow < lax.axis_size("gx") * rows))[:, None] & (
        (gcol >= 0) & (gcol < columns * cols)
    )[None, :]).astype(jnp.float32)

    kernel = lambda *refs: steps_kernel(*refs, levels=levels, at=at)
    return pl.pallas_call(
        kernel,
        out_shape=jax.ShapeDtypeStruct((2, levels, rows, cols), jnp.float32),
        scratch_shapes=[
            pltpu.VMEM((2 * levels, rows + 2 * h, lanes), jnp.float32),
            pltpu.VMEM((levels, rows + 2 * h, lanes), jnp.float32),
            pltpu.VMEM((levels, rows + 2 * h, lanes), jnp.float32),
        ],
    )(ext, inj, valid)


def solution(mesh):
    in_specs = (
        P(None, None, "gx", "gy"),
        P(None, "gx", "gy"),
        P(None, "gx", "gy"),
        P(None, "gx", "gy"),
        P("gx", "gy"),
        P(("gx", "gy"), None),
        P(("gx", "gy")),
        P(("gx", "gy")),
        P(("gx", "gy")),
    )
    out_specs = P(None, None, "gx", "gy")
    return jax.shard_map(
        on_device, mesh=mesh, in_specs=in_specs, out_specs=out_specs, check_vma=False
    )
```

```python
import jax
import jax.numpy as jnp
from jax import lax
from jax.sharding import PartitionSpec as P
from jax.experimental import pallas as pl
from jax.experimental.pallas import tpu as pltpu

LEV = 16
STEPS = 4
PR = 16
CAP = 8
HALO = STEPS


def from_behind(value, axis, steps):
    count = lax.axis_size(axis)
    initial, last = (max(0, -steps), min(count, count - steps))
    return lax.ppermute(value, axis, [(source, source + steps) for source in range(initial, last)])


def rows_halo(band, h):
    r = band.shape[1]
    below = from_behind(band[:, :h], "gx", -1)
    above = from_behind(band[:, r - h :], "gx", 1)
    return jnp.concatenate([band, below, above], axis=1)


def column_halo(a, h):
    c, r, w = a.shape
    left = from_behind(a[:, :, w - h:].reshape(c, r * h), "gy", 1).reshape(c, r, h)
    right = from_behind(a[:, :, :h].reshape(c, r * h), "gy", -1).reshape(c, r, h)
    return left, right


def with_halo(a, left, right, h, lanes):
    c, r, w = a.shape
    gap = jnp.zeros((c, r, lanes - w - 2 * h), a.dtype)
    return rows_halo(jnp.concatenate([a, right, gap, left], axis=2), h)


def steps_kernel(ext_ref, inj_ref, valid_ref, o_ref, q_s, inv_s, sw_s, *, levels, at):
    rows_ext, lanes = valid_ref.shape
    rows, cols = o_ref.shape[2], o_ref.shape[3]
    for p in range(2 * levels):
        q_s[p] = ext_ref[p]
    valid = valid_ref[...] != 0.0
    keep = 1.0 - jnp.exp(-ext_ref[at["rate"]])
    sweep_prev = None
    for l in range(levels):
        diag = jnp.ones((rows_ext, lanes), jnp.float32)
        if l >= 1:
            diag = diag + ext_ref[at["kd"] + l - 1]
        if l < levels - 1:
            diag = diag + ext_ref[at["kd"] + l]
        if l == 0:
            denom = diag
        else:
            denom = diag - (-ext_ref[at["kd"] + l - 1]) * sweep_prev
        inv_here = 1.0 / denom
        inv_s[l] = inv_here
        if l < levels - 1:
            sweep_prev = (-ext_ref[at["kd"] + l]) * inv_here
            sw_s[l] = sweep_prev
    zero = jnp.zeros((rows_ext, lanes), jnp.float32)

    def one_step(step, carry):
        def forward(l, prev):
            p0, p1 = prev
            wxl = ext_ref[at["wx"] + l]
            wyl = ext_ref[at["wy"] + l]
            out_x = jnp.maximum(wxl, 0.0)
            in_x = jnp.minimum(wxl, 0.0)
            out_y = jnp.maximum(wyl, 0.0)
            in_y = jnp.minimum(wyl, 0.0)

            def advect(x):
                flux_x = out_x * x + in_x * pltpu.roll(x, rows_ext - 1, 0)
                flux_y = out_y * x + in_y * pltpu.roll(x, lanes - 1, 1)
                return x - (flux_x - pltpu.roll(flux_x, 1, 0)) - (flux_y - pltpu.roll(flux_y, 1, 1))

            a0 = advect(q_s[l])
            a1 = advect(q_s[levels + l])
            so2 = a0 + inj_ref[l]
            loss = so2 * keep
            c0 = so2 - loss
            c1 = a1 + 1.5 * loss
            inv = inv_s[l]
            lower = -ext_ref[at["kd"] + jnp.maximum(l - 1, 0)]
            f0 = (c0 - lower * p0) * inv
            f1 = (c1 - lower * p1) * inv
            q_s[l] = f0
            q_s[levels + l] = f1
            return (f0, f1)

        f0, f1 = lax.fori_loop(0, levels, forward, (zero, zero), unroll=True)
        q_s[levels - 1] = jnp.where(valid, f0, 0.0)
        q_s[2 * levels - 1] = jnp.where(valid, f1, 0.0)

        def backward(i, nxt):
            l = levels - 2 - i
            n0, n1 = nxt
            sw = sw_s[l]
            r0 = q_s[l] - sw * n0
            r1 = q_s[levels + l] - sw * n1
            q_s[l] = jnp.where(valid, r0, 0.0)
            q_s[levels + l] = jnp.where(valid, r1, 0.0)
            return (r0, r1)

        lax.fori_loop(0, levels - 1, backward, (f0, f1), unroll=True)
        return carry

    lax.fori_loop(0, STEPS, one_step, 0)
    for p in range(2 * levels):
        o_ref[p // levels, p % levels] = q_s[p, 0:rows, 0:cols]


def thomas_factor(kdiff):
    levels = kdiff.shape[0] + 1
    lower = []
    upper = []
    diag = []
    for l in range(levels):
        d_here = jnp.ones_like(kdiff[0])
        if l >= 1:
            d_here = d_here + kdiff[l - 1]
            lower.append(-kdiff[l - 1])
        else:
            lower.append(jnp.zeros_like(kdiff[0]))
        if l < levels - 1:
            d_here = d_here + kdiff[l]
            upper.append(-kdiff[l])
        else:
            upper.append(jnp.zeros_like(kdiff[0]))
        diag.append(d_here)
    inverse = []
    sweep = []
    for l in range(levels):
        if l == 0:
            denom = diag[0]
        else:
            denom = diag[l] - lower[l] * sweep[l - 1]
        inv_here = 1.0 / denom
        inverse.append(inv_here)
        sweep.append(upper[l] * inv_here)
    return (lower, inverse, sweep)


def thomas_solve(rhs, factors):
    lower, inverse, sweep = factors
    levels = len(inverse)
    forward = []
    for l in range(levels):
        if l == 0:
            forward.append(rhs[:, 0] * inverse[0])
        else:
            forward.append((rhs[:, l] - lower[l] * forward[l - 1]) * inverse[l])
    result = [None] * levels
    result[levels - 1] = forward[levels - 1]
    for l in range(levels - 2, -1, -1):
        result[l] = forward[l] - sweep[l] * result[l + 1]
    return jnp.stack(result, axis=1)


def upwind(courant, here, ahead):
    return jnp.maximum(courant, 0.0) * here + jnp.minimum(courant, 0.0) * ahead


def plume_matrix(blocks, row_f, top_f, positions):
    levels = jnp.arange(LEV, dtype=jnp.float32)
    weight = jnp.where(
        levels[None, :] < top_f[:, None], 1.0 / jnp.maximum(top_f, 1.0)[:, None], jnp.float32(0.0)
    )
    place = (row_f[:, None] == jnp.arange(positions, dtype=jnp.float32)[None, :]).astype(
        jnp.float32
    )
    mixed = (weight[:, :, None] * place[:, None, :]).reshape(blocks.shape[0], LEV * positions)
    return jnp.dot(
        mixed.T, blocks, precision=lax.Precision.HIGHEST, preferred_element_type=jnp.float32
    )


def on_device(tracers, wind_x, wind_y, kdiff, rate, seg_blocks, seg_target, seg_row, seg_top):
    rows = tracers.shape[2]
    cols = tracers.shape[3]
    levels = tracers.shape[1]
    positions = rows // PR
    count = seg_target.shape[0]
    width = seg_blocks.shape[1]
    h = HALO
    row_f = seg_row.astype(jnp.float32)
    top_f = seg_top.astype(jnp.float32)
    columns = lax.axis_size("gy")
    order = jnp.arange(count, dtype=jnp.int32)
    same = seg_target[:, None] == seg_target[None, :]
    rank = jnp.sum((same & (order[:, None] < order[None, :])).astype(jnp.int32), axis=0)
    slot = seg_target * CAP + rank
    place = (slot[:, None] == jnp.arange(columns * CAP, dtype=jnp.int32)[None, :]).astype(
        jnp.float32
    )
    payload = jnp.concatenate([seg_blocks, row_f[:, None], top_f[:, None]], axis=1)
    outgoing = jnp.dot(
        place.T, payload, precision=lax.Precision.HIGHEST, preferred_element_type=jnp.float32
    )
    main = outgoing.reshape(columns, CAP, width + 2)
    details = main[:, :, width:]
    shaped = main[:, :, :width].reshape(columns, CAP, PR, cols)
    tail_cols = jnp.concatenate([shaped[:, :, :, cols - h:].reshape(columns, CAP, PR * h), details], axis=2)
    head_cols = jnp.concatenate([shaped[:, :, :, :h].reshape(columns, CAP, PR * h), details], axis=2)
    empty = jnp.zeros_like(tail_cols[:1])
    to_left_halo = jnp.concatenate([empty, tail_cols[:-1]], axis=0)
    to_right_halo = jnp.concatenate([head_cols[1:], empty], axis=0)
    edge = PR * h + 2
    lanes = -(-(cols + 2 * h) // 128) * 128
    packed = jnp.concatenate(
        [tracers.reshape(2 * levels, rows, cols), wind_x, wind_y, kdiff, rate[None]], axis=0
    )
    left_cols, right_cols = column_halo(packed, h)
    sendable, left_cols, right_cols = lax.optimization_barrier(
        (jnp.concatenate([main, to_left_halo, to_right_halo], axis=2), left_cols, right_cols)
    )
    arrived = lax.all_to_all(
        sendable,
        "gy",
        split_axis=0,
        concat_axis=0,
        tiled=True,
    ).reshape(columns * CAP, width + 2 + 2 * edge)

    ext = with_halo(packed, left_cols, right_cols, h, lanes)

    def injected(part, span):
        plume = plume_matrix(part[:, : PR * span], part[:, PR * span], part[:, PR * span + 1], positions)
        return plume.reshape(LEV, positions, PR, span).reshape(LEV, rows, span)

    injection = injected(arrived[:, : width + 2], cols)
    left = injected(arrived[:, width + 2 : width + 2 + edge], h)
    right = injected(arrived[:, width + 2 + edge :], h)
    gap = jnp.zeros((LEV, rows, lanes - cols - 2 * h), jnp.float32)
    band = jnp.concatenate([injection, right, gap, left], axis=2)
    inj = rows_halo(band, h)
    at = {"wx": 2 * levels}
    at["wy"] = at["wx"] + levels
    at["kd"] = at["wy"] + levels
    at["rate"] = at["kd"] + levels - 1

    gi = lax.axis_index("gx")
    gj = lax.axis_index("gy")
    rpos = jnp.arange(rows + 2 * h, dtype=jnp.int32)
    rpos = jnp.where(rpos < rows + h, rpos, rpos - (rows + 2 * h))
    lpos = jnp.arange(lanes, dtype=jnp.int32)
    lpos = jnp.where(lpos < cols + h, lpos, jnp.where(lpos >= lanes - h, lpos - lanes, -(cols * columns + 1)))
    grow = gi * rows + rpos
    gcol = gj * cols + lpos
    valid = (((grow >= 0) & (grow < lax.axis_size("gx") * rows))[:, None] & (
        (gcol >= 0) & (gcol < columns * cols)
    )[None, :]).astype(jnp.float32)

    kernel = lambda *refs: steps_kernel(*refs, levels=levels, at=at)
    return pl.pallas_call(
        kernel,
        out_shape=jax.ShapeDtypeStruct((2, levels, rows, cols), jnp.float32),
        scratch_shapes=[
            pltpu.VMEM((2 * levels, rows + 2 * h, lanes), jnp.float32),
            pltpu.VMEM((levels, rows + 2 * h, lanes), jnp.float32),
            pltpu.VMEM((levels, rows + 2 * h, lanes), jnp.float32),
        ],
    )(ext, inj, valid)


def solution(mesh):
    in_specs = (
        P(None, None, "gx", "gy"),
        P(None, "gx", "gy"),
        P(None, "gx", "gy"),
        P(None, "gx", "gy"),
        P("gx", "gy"),
        P(("gx", "gy"), None),
        P(("gx", "gy")),
        P(("gx", "gy")),
        P(("gx", "gy")),
    )
    out_specs = P(None, None, "gx", "gy")
    return jax.shard_map(
        on_device, mesh=mesh, in_specs=in_specs, out_specs=out_specs, check_vma=False
    )
```

```python
import jax
import jax.numpy as jnp
from jax import lax
from jax.sharding import PartitionSpec as P
from jax.experimental import pallas as pl
from jax.experimental.pallas import tpu as pltpu

LEV = 16
STEPS = 4
PR = 16
CAP = 8
HALO = STEPS


def from_behind(value, axis, steps):
    count = lax.axis_size(axis)
    initial, last = (max(0, -steps), min(count, count - steps))
    return lax.ppermute(value, axis, [(source, source + steps) for source in range(initial, last)])


def rows_halo(band, h):
    r = band.shape[1]
    below = from_behind(band[:, :h], "gx", -1)
    above = from_behind(band[:, r - h :], "gx", 1)
    return jnp.concatenate([band, below, above], axis=1)


def column_halo(a, h):
    c, r, w = a.shape
    left = from_behind(a[:, :, w - h:].reshape(c, r * h), "gy", 1).reshape(c, r, h)
    right = from_behind(a[:, :, :h].reshape(c, r * h), "gy", -1).reshape(c, r, h)
    return left, right


def with_halo(a, left, right, h, lanes):
    c, r, w = a.shape
    gap = jnp.zeros((c, r, lanes - w - 2 * h), a.dtype)
    return rows_halo(jnp.concatenate([a, right, gap, left], axis=2), h)


def steps_kernel(ext_ref, inj_ref, valid_ref, o_ref, q_s, inv_s, sw_s, *, levels, at):
    rows_ext, lanes = valid_ref.shape
    rows, cols = o_ref.shape[2], o_ref.shape[3]
    for p in range(2 * levels):
        q_s[p] = ext_ref[p]
    valid = valid_ref[...] != 0.0
    keep = 1.0 - jnp.exp(-ext_ref[at["rate"]])
    sweep_prev = None
    for l in range(levels):
        diag = jnp.ones((rows_ext, lanes), jnp.float32)
        if l >= 1:
            diag = diag + ext_ref[at["kd"] + l - 1]
        if l < levels - 1:
            diag = diag + ext_ref[at["kd"] + l]
        if l == 0:
            denom = diag
        else:
            denom = diag - (-ext_ref[at["kd"] + l - 1]) * sweep_prev
        inv_here = 1.0 / denom
        inv_s[l] = inv_here
        if l < levels - 1:
            sweep_prev = (-ext_ref[at["kd"] + l]) * inv_here
            sw_s[l] = sweep_prev
    zero = jnp.zeros((rows_ext, lanes), jnp.float32)

    def one_step(step, carry):
        def forward(l, prev):
            p0, p1 = prev
            wxl = ext_ref[at["wx"] + l]
            wyl = ext_ref[at["wy"] + l]
            out_x = jnp.maximum(wxl, 0.0)
            in_x = jnp.minimum(wxl, 0.0)
            out_y = jnp.maximum(wyl, 0.0)
            in_y = jnp.minimum(wyl, 0.0)

            def advect(x):
                flux_x = out_x * x + in_x * pltpu.roll(x, rows_ext - 1, 0)
                flux_y = out_y * x + in_y * pltpu.roll(x, lanes - 1, 1)
                return x - (flux_x - pltpu.roll(flux_x, 1, 0)) - (flux_y - pltpu.roll(flux_y, 1, 1))

            a0 = advect(q_s[l])
            a1 = advect(q_s[levels + l])
            so2 = a0 + inj_ref[l]
            loss = so2 * keep
            c0 = so2 - loss
            c1 = a1 + 1.5 * loss
            inv = inv_s[l]
            lower = -ext_ref[at["kd"] + jnp.maximum(l - 1, 0)]
            f0 = (c0 - lower * p0) * inv
            f1 = (c1 - lower * p1) * inv
            q_s[l] = f0
            q_s[levels + l] = f1
            return (f0, f1)

        f0, f1 = lax.fori_loop(0, levels, forward, (zero, zero), unroll=True)
        q_s[levels - 1] = jnp.where(valid, f0, 0.0)
        q_s[2 * levels - 1] = jnp.where(valid, f1, 0.0)

        def backward(i, nxt):
            l = levels - 2 - i
            n0, n1 = nxt
            sw = sw_s[l]
            r0 = q_s[l] - sw * n0
            r1 = q_s[levels + l] - sw * n1
            q_s[l] = jnp.where(valid, r0, 0.0)
            q_s[levels + l] = jnp.where(valid, r1, 0.0)
            return (r0, r1)

        lax.fori_loop(0, levels - 1, backward, (f0, f1), unroll=True)
        return carry

    lax.fori_loop(0, STEPS, one_step, 0)
    for p in range(2 * levels):
        o_ref[p // levels, p % levels] = q_s[p, 0:rows, 0:cols]


def thomas_factor(kdiff):
    levels = kdiff.shape[0] + 1
    lower = []
    upper = []
    diag = []
    for l in range(levels):
        d_here = jnp.ones_like(kdiff[0])
        if l >= 1:
            d_here = d_here + kdiff[l - 1]
            lower.append(-kdiff[l - 1])
        else:
            lower.append(jnp.zeros_like(kdiff[0]))
        if l < levels - 1:
            d_here = d_here + kdiff[l]
            upper.append(-kdiff[l])
        else:
            upper.append(jnp.zeros_like(kdiff[0]))
        diag.append(d_here)
    inverse = []
    sweep = []
    for l in range(levels):
        if l == 0:
            denom = diag[0]
        else:
            denom = diag[l] - lower[l] * sweep[l - 1]
        inv_here = 1.0 / denom
        inverse.append(inv_here)
        sweep.append(upper[l] * inv_here)
    return (lower, inverse, sweep)


def thomas_solve(rhs, factors):
    lower, inverse, sweep = factors
    levels = len(inverse)
    forward = []
    for l in range(levels):
        if l == 0:
            forward.append(rhs[:, 0] * inverse[0])
        else:
            forward.append((rhs[:, l] - lower[l] * forward[l - 1]) * inverse[l])
    result = [None] * levels
    result[levels - 1] = forward[levels - 1]
    for l in range(levels - 2, -1, -1):
        result[l] = forward[l] - sweep[l] * result[l + 1]
    return jnp.stack(result, axis=1)


def upwind(courant, here, ahead):
    return jnp.maximum(courant, 0.0) * here + jnp.minimum(courant, 0.0) * ahead


def plume_matrix(blocks, row_f, top_f, positions):
    levels = jnp.arange(LEV, dtype=jnp.float32)
    weight = jnp.where(
        levels[None, :] < top_f[:, None], 1.0 / jnp.maximum(top_f, 1.0)[:, None], jnp.float32(0.0)
    )
    place = (row_f[:, None] == jnp.arange(positions, dtype=jnp.float32)[None, :]).astype(
        jnp.float32
    )
    mixed = (weight[:, :, None] * place[:, None, :]).reshape(blocks.shape[0], LEV * positions)
    return jnp.dot(
        mixed.T, blocks, precision=lax.Precision.HIGHEST, preferred_element_type=jnp.float32
    )


def on_device(tracers, wind_x, wind_y, kdiff, rate, seg_blocks, seg_target, seg_row, seg_top):
    rows = tracers.shape[2]
    cols = tracers.shape[3]
    levels = tracers.shape[1]
    positions = rows // PR
    count = seg_target.shape[0]
    width = seg_blocks.shape[1]
    h = HALO
    row_f = seg_row.astype(jnp.float32)
    top_f = seg_top.astype(jnp.float32)
    columns = lax.axis_size("gy")
    order = jnp.arange(count, dtype=jnp.int32)
    same = seg_target[:, None] == seg_target[None, :]
    rank = jnp.sum((same & (order[:, None] < order[None, :])).astype(jnp.int32), axis=0)
    strip = PR * h
    blocks3 = seg_blocks.reshape(count, PR, cols)
    tail = blocks3[:, :, cols - h :].reshape(count, strip)
    head = blocks3[:, :, :h].reshape(count, strip)
    det = jnp.stack([row_f, top_f], axis=1)
    det_at = width + 2 * strip
    wide = det_at + 6

    def pad(x, before, after):
        return jnp.pad(x, ((0, 0), (before, after)))

    payload = jnp.concatenate(
        [
            pad(jnp.concatenate([seg_blocks, pad(det, 2 * strip, 4)], axis=1), 0, 0),
            pad(jnp.concatenate([pad(tail, width, strip), pad(det, 2, 2)], axis=1), 0, 0),
            pad(jnp.concatenate([pad(head, width + strip, 0), pad(det, 4, 0)], axis=1), 0, 0),
        ],
        axis=0,
    )
    dest = jnp.concatenate(
        [seg_target * CAP + rank, (seg_target + 1) * CAP + rank, (seg_target - 1) * CAP + rank]
    )
    place = (dest[:, None] == jnp.arange(columns * CAP, dtype=jnp.int32)[None, :]).astype(
        jnp.float32
    )
    outgoing = jnp.dot(
        place.T, payload, precision=lax.Precision.HIGHEST, preferred_element_type=jnp.float32
    )
    lanes = -(-(cols + 2 * h) // 128) * 128
    packed = jnp.concatenate(
        [tracers.reshape(2 * levels, rows, cols), wind_x, wind_y, kdiff, rate[None]], axis=0
    )
    left_cols, right_cols = column_halo(packed, h)
    sendable, left_cols, right_cols = lax.optimization_barrier(
        (outgoing.reshape(columns, CAP, wide), left_cols, right_cols)
    )
    arrived = lax.all_to_all(
        sendable,
        "gy",
        split_axis=0,
        concat_axis=0,
        tiled=True,
    ).reshape(columns * CAP, wide)

    ext = with_halo(packed, left_cols, right_cols, h, lanes)

    def injected(lo, span, d):
        part = arrived[:, lo : lo + PR * span]
        plume = plume_matrix(part, arrived[:, det_at + d], arrived[:, det_at + d + 1], positions)
        return plume.reshape(LEV, positions, PR, span).reshape(LEV, rows, span)

    injection = injected(0, cols, 0)
    left = injected(width, h, 2)
    right = injected(width + strip, h, 4)
    gap = jnp.zeros((LEV, rows, lanes - cols - 2 * h), jnp.float32)
    band = jnp.concatenate([injection, right, gap, left], axis=2)
    inj = rows_halo(band, h)
    at = {"wx": 2 * levels}
    at["wy"] = at["wx"] + levels
    at["kd"] = at["wy"] + levels
    at["rate"] = at["kd"] + levels - 1

    gi = lax.axis_index("gx")
    gj = lax.axis_index("gy")
    rpos = jnp.arange(rows + 2 * h, dtype=jnp.int32)
    rpos = jnp.where(rpos < rows + h, rpos, rpos - (rows + 2 * h))
    lpos = jnp.arange(lanes, dtype=jnp.int32)
    lpos = jnp.where(lpos < cols + h, lpos, jnp.where(lpos >= lanes - h, lpos - lanes, -(cols * columns + 1)))
    grow = gi * rows + rpos
    gcol = gj * cols + lpos
    valid = (((grow >= 0) & (grow < lax.axis_size("gx") * rows))[:, None] & (
        (gcol >= 0) & (gcol < columns * cols)
    )[None, :]).astype(jnp.float32)

    kernel = lambda *refs: steps_kernel(*refs, levels=levels, at=at)
    return pl.pallas_call(
        kernel,
        out_shape=jax.ShapeDtypeStruct((2, levels, rows, cols), jnp.float32),
        scratch_shapes=[
            pltpu.VMEM((2 * levels, rows + 2 * h, lanes), jnp.float32),
            pltpu.VMEM((levels, rows + 2 * h, lanes), jnp.float32),
            pltpu.VMEM((levels, rows + 2 * h, lanes), jnp.float32),
        ],
    )(ext, inj, valid)


def solution(mesh):
    in_specs = (
        P(None, None, "gx", "gy"),
        P(None, "gx", "gy"),
        P(None, "gx", "gy"),
        P(None, "gx", "gy"),
        P("gx", "gy"),
        P(("gx", "gy"), None),
        P(("gx", "gy")),
        P(("gx", "gy")),
        P(("gx", "gy")),
    )
    out_specs = P(None, None, "gx", "gy")
    return jax.shard_map(
        on_device, mesh=mesh, in_specs=in_specs, out_specs=out_specs, check_vma=False
    )
```

```python
import jax
import jax.numpy as jnp
from jax import lax
from jax.sharding import PartitionSpec as P
from jax.experimental import pallas as pl
from jax.experimental.pallas import tpu as pltpu

LEV = 16
STEPS = 4
PR = 16
CAP = 8
HALO = STEPS


def from_behind(value, axis, steps):
    count = lax.axis_size(axis)
    initial, last = (max(0, -steps), min(count, count - steps))
    return lax.ppermute(value, axis, [(source, source + steps) for source in range(initial, last)])


def rows_halo(band, h):
    r = band.shape[1]
    below = from_behind(band[:, :h], "gx", -1)
    above = from_behind(band[:, r - h :], "gx", 1)
    return jnp.concatenate([band, below, above], axis=1)


def column_halo(a, h):
    c, r, w = a.shape
    left = from_behind(a[:, :, w - h:].reshape(c, r * h), "gy", 1).reshape(c, r, h)
    right = from_behind(a[:, :, :h].reshape(c, r * h), "gy", -1).reshape(c, r, h)
    return left, right


def with_halo(a, left, right, h, lanes):
    c, r, w = a.shape
    gap = jnp.zeros((c, r, lanes - w - 2 * h), a.dtype)
    return rows_halo(jnp.concatenate([a, right, gap, left], axis=2), h)


def steps_kernel(ext_ref, inj_ref, valid_ref, o_ref, q_s, inv_s, sw_s, *, levels, at):
    rows_ext, lanes = valid_ref.shape
    rows, cols = o_ref.shape[2], o_ref.shape[3]
    for p in range(2 * levels):
        q_s[p] = ext_ref[p]
    valid = valid_ref[...] != 0.0
    keep = 1.0 - jnp.exp(-ext_ref[at["rate"]])
    sweep_prev = None
    for l in range(levels):
        diag = jnp.ones((rows_ext, lanes), jnp.float32)
        if l >= 1:
            diag = diag + ext_ref[at["kd"] + l - 1]
        if l < levels - 1:
            diag = diag + ext_ref[at["kd"] + l]
        if l == 0:
            denom = diag
        else:
            denom = diag - (-ext_ref[at["kd"] + l - 1]) * sweep_prev
        inv_here = 1.0 / denom
        inv_s[l] = inv_here
        if l < levels - 1:
            sweep_prev = (-ext_ref[at["kd"] + l]) * inv_here
            sw_s[l] = sweep_prev
    zero = jnp.zeros((rows_ext, lanes), jnp.float32)

    def one_step(step, carry):
        def forward(l, prev):
            p0, p1 = prev
            wxl = ext_ref[at["wx"] + l]
            wyl = ext_ref[at["wy"] + l]
            out_x = jnp.maximum(wxl, 0.0)
            in_x = jnp.minimum(wxl, 0.0)
            out_y = jnp.maximum(wyl, 0.0)
            in_y = jnp.minimum(wyl, 0.0)

            def advect(x):
                flux_x = out_x * x + in_x * pltpu.roll(x, rows_ext - 1, 0)
                flux_y = out_y * x + in_y * pltpu.roll(x, lanes - 1, 1)
                return x - (flux_x - pltpu.roll(flux_x, 1, 0)) - (flux_y - pltpu.roll(flux_y, 1, 1))

            a0 = advect(q_s[l])
            a1 = advect(q_s[levels + l])
            so2 = a0 + inj_ref[l]
            loss = so2 * keep
            c0 = so2 - loss
            c1 = a1 + 1.5 * loss
            inv = inv_s[l]
            lower = -ext_ref[at["kd"] + jnp.maximum(l - 1, 0)]
            f0 = (c0 - lower * p0) * inv
            f1 = (c1 - lower * p1) * inv
            q_s[l] = f0
            q_s[levels + l] = f1
            return (f0, f1)

        f0, f1 = lax.fori_loop(0, levels, forward, (zero, zero), unroll=True)
        q_s[levels - 1] = jnp.where(valid, f0, 0.0)
        q_s[2 * levels - 1] = jnp.where(valid, f1, 0.0)

        def backward(i, nxt):
            l = levels - 2 - i
            n0, n1 = nxt
            sw = sw_s[l]
            r0 = q_s[l] - sw * n0
            r1 = q_s[levels + l] - sw * n1
            q_s[l] = jnp.where(valid, r0, 0.0)
            q_s[levels + l] = jnp.where(valid, r1, 0.0)
            return (r0, r1)

        lax.fori_loop(0, levels - 1, backward, (f0, f1), unroll=True)
        return carry

    lax.fori_loop(0, STEPS, one_step, 0)
    for p in range(2 * levels):
        o_ref[p // levels, p % levels] = q_s[p, 0:rows, 0:cols]


def thomas_factor(kdiff):
    levels = kdiff.shape[0] + 1
    lower = []
    upper = []
    diag = []
    for l in range(levels):
        d_here = jnp.ones_like(kdiff[0])
        if l >= 1:
            d_here = d_here + kdiff[l - 1]
            lower.append(-kdiff[l - 1])
        else:
            lower.append(jnp.zeros_like(kdiff[0]))
        if l < levels - 1:
            d_here = d_here + kdiff[l]
            upper.append(-kdiff[l])
        else:
            upper.append(jnp.zeros_like(kdiff[0]))
        diag.append(d_here)
    inverse = []
    sweep = []
    for l in range(levels):
        if l == 0:
            denom = diag[0]
        else:
            denom = diag[l] - lower[l] * sweep[l - 1]
        inv_here = 1.0 / denom
        inverse.append(inv_here)
        sweep.append(upper[l] * inv_here)
    return (lower, inverse, sweep)


def thomas_solve(rhs, factors):
    lower, inverse, sweep = factors
    levels = len(inverse)
    forward = []
    for l in range(levels):
        if l == 0:
            forward.append(rhs[:, 0] * inverse[0])
        else:
            forward.append((rhs[:, l] - lower[l] * forward[l - 1]) * inverse[l])
    result = [None] * levels
    result[levels - 1] = forward[levels - 1]
    for l in range(levels - 2, -1, -1):
        result[l] = forward[l] - sweep[l] * result[l + 1]
    return jnp.stack(result, axis=1)


def upwind(courant, here, ahead):
    return jnp.maximum(courant, 0.0) * here + jnp.minimum(courant, 0.0) * ahead


def plume_matrix(blocks, row_f, top_f, positions):
    levels = jnp.arange(LEV, dtype=jnp.float32)
    weight = jnp.where(
        levels[None, :] < top_f[:, None], 1.0 / jnp.maximum(top_f, 1.0)[:, None], jnp.float32(0.0)
    )
    place = (row_f[:, None] == jnp.arange(positions, dtype=jnp.float32)[None, :]).astype(
        jnp.float32
    )
    mixed = (weight[:, :, None] * place[:, None, :]).reshape(blocks.shape[0], LEV * positions)
    return jnp.dot(
        mixed.T, blocks, precision=lax.Precision.HIGHEST, preferred_element_type=jnp.float32
    )


def on_device(tracers, wind_x, wind_y, kdiff, rate, seg_blocks, seg_target, seg_row, seg_top):
    rows = tracers.shape[2]
    cols = tracers.shape[3]
    levels = tracers.shape[1]
    positions = rows // PR
    count = seg_target.shape[0]
    width = seg_blocks.shape[1]
    h = HALO
    row_f = seg_row.astype(jnp.float32)
    top_f = seg_top.astype(jnp.float32)
    columns = lax.axis_size("gy")
    order = jnp.arange(count, dtype=jnp.int32)
    same = seg_target[:, None] == seg_target[None, :]
    rank = jnp.sum((same & (order[:, None] < order[None, :])).astype(jnp.int32), axis=0)
    strip = PR * h
    blocks3 = seg_blocks.reshape(count, PR, cols)
    tail = blocks3[:, :, cols - h :].reshape(count, strip)
    head = blocks3[:, :, :h].reshape(count, strip)
    det = jnp.stack([row_f, top_f], axis=1)
    det_at = width + 2 * strip
    wide = det_at + 6

    def pad(x, before, after):
        return jnp.pad(x, ((0, 0), (before, after)))

    payload = jnp.concatenate(
        [
            pad(jnp.concatenate([seg_blocks, pad(det, 2 * strip, 4)], axis=1), 0, 0),
            pad(jnp.concatenate([pad(tail, width, strip), pad(det, 2, 2)], axis=1), 0, 0),
            pad(jnp.concatenate([pad(head, width + strip, 0), pad(det, 4, 0)], axis=1), 0, 0),
        ],
        axis=0,
    )
    dest = jnp.concatenate(
        [seg_target * CAP + rank, (seg_target + 1) * CAP + rank, (seg_target - 1) * CAP + rank]
    )
    place = (dest[:, None] == jnp.arange(columns * CAP, dtype=jnp.int32)[None, :]).astype(
        jnp.float32
    )
    outgoing = jnp.dot(
        place.T, payload, precision=lax.Precision.HIGHEST, preferred_element_type=jnp.float32
    )
    lanes = -(-(cols + 2 * h) // 128) * 128
    packed = jnp.concatenate(
        [tracers.reshape(2 * levels, rows, cols), wind_x, wind_y, kdiff, rate[None]], axis=0
    )
    left_cols, right_cols = column_halo(packed, h)
    sendable, left_cols, right_cols = lax.optimization_barrier(
        (outgoing.reshape(columns, CAP, wide), left_cols, right_cols)
    )
    arrived = lax.all_to_all(
        sendable,
        "gy",
        split_axis=0,
        concat_axis=0,
        tiled=True,
    ).reshape(columns * CAP, wide)

    ext = with_halo(packed, left_cols, right_cols, h, lanes)
    ext, arrived = lax.optimization_barrier((ext, arrived))

    levels_f = jnp.arange(LEV, dtype=jnp.float32)

    def mixing(d):
        row_here = arrived[:, det_at + d]
        top_here = arrived[:, det_at + d + 1]
        weight = jnp.where(
            levels_f[None, :] < top_here[:, None], 1.0 / jnp.maximum(top_here, 1.0)[:, None], jnp.float32(0.0)
        )
        at_row = (row_here[:, None] == jnp.arange(positions, dtype=jnp.float32)[None, :]).astype(jnp.float32)
        return (weight[:, :, None] * at_row[:, None, :]).reshape(arrived.shape[0], LEV * positions)

    mixed = jnp.concatenate([mixing(0), mixing(2), mixing(4)], axis=1)
    plume = jnp.dot(
        mixed.T, arrived[:, :det_at], precision=lax.Precision.HIGHEST, preferred_element_type=jnp.float32
    )
    share = LEV * positions

    def injected(group, lo, span):
        part = plume[group * share : (group + 1) * share, lo : lo + PR * span]
        return part.reshape(LEV, positions, PR, span).reshape(LEV, rows, span)

    injection = injected(0, 0, cols)
    left = injected(1, width, h)
    right = injected(2, width + strip, h)
    gap = jnp.zeros((LEV, rows, lanes - cols - 2 * h), jnp.float32)
    band = jnp.concatenate([injection, right, gap, left], axis=2)
    inj = rows_halo(band, h)
    at = {"wx": 2 * levels}
    at["wy"] = at["wx"] + levels
    at["kd"] = at["wy"] + levels
    at["rate"] = at["kd"] + levels - 1

    gi = lax.axis_index("gx")
    gj = lax.axis_index("gy")
    rpos = jnp.arange(rows + 2 * h, dtype=jnp.int32)
    rpos = jnp.where(rpos < rows + h, rpos, rpos - (rows + 2 * h))
    lpos = jnp.arange(lanes, dtype=jnp.int32)
    lpos = jnp.where(lpos < cols + h, lpos, jnp.where(lpos >= lanes - h, lpos - lanes, -(cols * columns + 1)))
    grow = gi * rows + rpos
    gcol = gj * cols + lpos
    valid = (((grow >= 0) & (grow < lax.axis_size("gx") * rows))[:, None] & (
        (gcol >= 0) & (gcol < columns * cols)
    )[None, :]).astype(jnp.float32)

    kernel = lambda *refs: steps_kernel(*refs, levels=levels, at=at)
    return pl.pallas_call(
        kernel,
        out_shape=jax.ShapeDtypeStruct((2, levels, rows, cols), jnp.float32),
        scratch_shapes=[
            pltpu.VMEM((2 * levels, rows + 2 * h, lanes), jnp.float32),
            pltpu.VMEM((levels, rows + 2 * h, lanes), jnp.float32),
            pltpu.VMEM((levels, rows + 2 * h, lanes), jnp.float32),
        ],
    )(ext, inj, valid)


def solution(mesh):
    in_specs = (
        P(None, None, "gx", "gy"),
        P(None, "gx", "gy"),
        P(None, "gx", "gy"),
        P(None, "gx", "gy"),
        P("gx", "gy"),
        P(("gx", "gy"), None),
        P(("gx", "gy")),
        P(("gx", "gy")),
        P(("gx", "gy")),
    )
    out_specs = P(None, None, "gx", "gy")
    return jax.shard_map(
        on_device, mesh=mesh, in_specs=in_specs, out_specs=out_specs, check_vma=False
    )
```

```python
import jax
import jax.numpy as jnp
from jax import lax
from jax.sharding import PartitionSpec as P
from jax.experimental import pallas as pl
from jax.experimental.pallas import tpu as pltpu

LEV = 16
STEPS = 4
PR = 16
CAP = 8
HALO = STEPS


def from_behind(value, axis, steps):
    count = lax.axis_size(axis)
    initial, last = (max(0, -steps), min(count, count - steps))
    return lax.ppermute(value, axis, [(source, source + steps) for source in range(initial, last)])


def rows_halo(band, h):
    r = band.shape[1]
    below = from_behind(band[:, :h], "gx", -1)
    above = from_behind(band[:, r - h :], "gx", 1)
    return jnp.concatenate([band, below, above], axis=1)


def column_halo(a, h):
    c, r, w = a.shape
    left = from_behind(a[:, :, w - h:].reshape(c, r * h), "gy", 1).reshape(c, r, h)
    right = from_behind(a[:, :, :h].reshape(c, r * h), "gy", -1).reshape(c, r, h)
    return left, right


def with_halo(a, left, right, h, lanes):
    c, r, w = a.shape
    gap = jnp.zeros((c, r, lanes - w - 2 * h), a.dtype)
    return rows_halo(jnp.concatenate([a, right, gap, left], axis=2), h)


def steps_kernel(ext_ref, inj_ref, valid_ref, o_ref, q_s, inv_s, sw_s, *, levels, at):
    rows_ext, lanes = valid_ref.shape
    rows, cols = o_ref.shape[2], o_ref.shape[3]
    for p in range(2 * levels):
        q_s[p] = ext_ref[p]
    valid = valid_ref[...] != 0.0
    keep = 1.0 - jnp.exp(-ext_ref[at["rate"]])
    sweep_prev = None
    for l in range(levels):
        diag = jnp.ones((rows_ext, lanes), jnp.float32)
        if l >= 1:
            diag = diag + ext_ref[at["kd"] + l - 1]
        if l < levels - 1:
            diag = diag + ext_ref[at["kd"] + l]
        if l == 0:
            denom = diag
        else:
            denom = diag - (-ext_ref[at["kd"] + l - 1]) * sweep_prev
        inv_here = 1.0 / denom
        inv_s[l] = inv_here
        if l < levels - 1:
            sweep_prev = (-ext_ref[at["kd"] + l]) * inv_here
            sw_s[l] = sweep_prev
    zero = jnp.zeros((rows_ext, lanes), jnp.float32)

    def one_step(step, carry):
        def forward(l, prev):
            p0, p1 = prev
            wxl = ext_ref[at["wx"] + l]
            wyl = ext_ref[at["wy"] + l]
            out_x = jnp.maximum(wxl, 0.0)
            in_x = jnp.minimum(wxl, 0.0)
            out_y = jnp.maximum(wyl, 0.0)
            in_y = jnp.minimum(wyl, 0.0)

            def advect(x):
                flux_x = out_x * x + in_x * pltpu.roll(x, rows_ext - 1, 0)
                flux_y = out_y * x + in_y * pltpu.roll(x, lanes - 1, 1)
                return x - (flux_x - pltpu.roll(flux_x, 1, 0)) - (flux_y - pltpu.roll(flux_y, 1, 1))

            a0 = advect(q_s[l])
            a1 = advect(q_s[levels + l])
            so2 = a0 + inj_ref[l]
            loss = so2 * keep
            c0 = so2 - loss
            c1 = a1 + 1.5 * loss
            inv = inv_s[l]
            lower = -ext_ref[at["kd"] + jnp.maximum(l - 1, 0)]
            f0 = (c0 - lower * p0) * inv
            f1 = (c1 - lower * p1) * inv
            q_s[l] = f0
            q_s[levels + l] = f1
            return (f0, f1)

        f0, f1 = lax.fori_loop(0, levels, forward, (zero, zero), unroll=True)
        q_s[levels - 1] = jnp.where(valid, f0, 0.0)
        q_s[2 * levels - 1] = jnp.where(valid, f1, 0.0)

        def backward(i, nxt):
            l = levels - 2 - i
            n0, n1 = nxt
            sw = sw_s[l]
            r0 = q_s[l] - sw * n0
            r1 = q_s[levels + l] - sw * n1
            q_s[l] = jnp.where(valid, r0, 0.0)
            q_s[levels + l] = jnp.where(valid, r1, 0.0)
            return (r0, r1)

        lax.fori_loop(0, levels - 1, backward, (f0, f1), unroll=True)
        return carry

    lax.fori_loop(0, STEPS, one_step, 0)
    for p in range(2 * levels):
        o_ref[p // levels, p % levels] = q_s[p, 0:rows, 0:cols]


def thomas_factor(kdiff):
    levels = kdiff.shape[0] + 1
    lower = []
    upper = []
    diag = []
    for l in range(levels):
        d_here = jnp.ones_like(kdiff[0])
        if l >= 1:
            d_here = d_here + kdiff[l - 1]
            lower.append(-kdiff[l - 1])
        else:
            lower.append(jnp.zeros_like(kdiff[0]))
        if l < levels - 1:
            d_here = d_here + kdiff[l]
            upper.append(-kdiff[l])
        else:
            upper.append(jnp.zeros_like(kdiff[0]))
        diag.append(d_here)
    inverse = []
    sweep = []
    for l in range(levels):
        if l == 0:
            denom = diag[0]
        else:
            denom = diag[l] - lower[l] * sweep[l - 1]
        inv_here = 1.0 / denom
        inverse.append(inv_here)
        sweep.append(upper[l] * inv_here)
    return (lower, inverse, sweep)


def thomas_solve(rhs, factors):
    lower, inverse, sweep = factors
    levels = len(inverse)
    forward = []
    for l in range(levels):
        if l == 0:
            forward.append(rhs[:, 0] * inverse[0])
        else:
            forward.append((rhs[:, l] - lower[l] * forward[l - 1]) * inverse[l])
    result = [None] * levels
    result[levels - 1] = forward[levels - 1]
    for l in range(levels - 2, -1, -1):
        result[l] = forward[l] - sweep[l] * result[l + 1]
    return jnp.stack(result, axis=1)


def upwind(courant, here, ahead):
    return jnp.maximum(courant, 0.0) * here + jnp.minimum(courant, 0.0) * ahead


def plume_matrix(blocks, row_f, top_f, positions):
    levels = jnp.arange(LEV, dtype=jnp.float32)
    weight = jnp.where(
        levels[None, :] < top_f[:, None], 1.0 / jnp.maximum(top_f, 1.0)[:, None], jnp.float32(0.0)
    )
    place = (row_f[:, None] == jnp.arange(positions, dtype=jnp.float32)[None, :]).astype(
        jnp.float32
    )
    mixed = (weight[:, :, None] * place[:, None, :]).reshape(blocks.shape[0], LEV * positions)
    return jnp.dot(
        mixed.T, blocks, precision=lax.Precision.HIGHEST, preferred_element_type=jnp.float32
    )


def on_device(tracers, wind_x, wind_y, kdiff, rate, seg_blocks, seg_target, seg_row, seg_top):
    rows = tracers.shape[2]
    cols = tracers.shape[3]
    levels = tracers.shape[1]
    positions = rows // PR
    count = seg_target.shape[0]
    width = seg_blocks.shape[1]
    h = HALO
    row_f = seg_row.astype(jnp.float32)
    top_f = seg_top.astype(jnp.float32)
    columns = lax.axis_size("gy")
    order = jnp.arange(count, dtype=jnp.int32)
    same = seg_target[:, None] == seg_target[None, :]
    rank = jnp.sum((same & (order[:, None] < order[None, :])).astype(jnp.int32), axis=0)
    strip = PR * h
    blocks3 = seg_blocks.reshape(count, PR, cols)
    tail = blocks3[:, :, cols - h :].reshape(count, strip)
    head = blocks3[:, :, :h].reshape(count, strip)
    det = jnp.stack([row_f, top_f], axis=1)
    det_at = width + 2 * strip
    wide = det_at + 6

    def pad(x, before, after):
        return jnp.pad(x, ((0, 0), (before, after)))

    payload = jnp.concatenate(
        [
            pad(jnp.concatenate([seg_blocks, pad(det, 2 * strip, 4)], axis=1), 0, 0),
            pad(jnp.concatenate([pad(tail, width, strip), pad(det, 2, 2)], axis=1), 0, 0),
            pad(jnp.concatenate([pad(head, width + strip, 0), pad(det, 4, 0)], axis=1), 0, 0),
        ],
        axis=0,
    )
    dest = jnp.concatenate(
        [seg_target * CAP + rank, (seg_target + 1) * CAP + rank, (seg_target - 1) * CAP + rank]
    )
    place = (dest[:, None] == jnp.arange(columns * CAP, dtype=jnp.int32)[None, :]).astype(
        jnp.float32
    )
    outgoing = jnp.dot(
        place.T, payload, precision=lax.Precision.HIGHEST, preferred_element_type=jnp.float32
    )
    lanes = -(-(cols + 2 * h) // 128) * 128
    packed = jnp.concatenate(
        [tracers.reshape(2 * levels, rows, cols), wind_x, wind_y, kdiff, rate[None]], axis=0
    )
    left_cols, right_cols = column_halo(packed, h)
    sendable, left_cols, right_cols = lax.optimization_barrier(
        (outgoing.reshape(columns, CAP, wide), left_cols, right_cols)
    )
    arrived = lax.all_to_all(
        sendable,
        "gy",
        split_axis=0,
        concat_axis=0,
        tiled=True,
    ).reshape(columns * CAP, wide)

    ext = with_halo(packed, left_cols, right_cols, h, lanes)

    levels_f = jnp.arange(LEV, dtype=jnp.float32)

    def mixing(d):
        row_here = arrived[:, det_at + d]
        top_here = arrived[:, det_at + d + 1]
        weight = jnp.where(
            levels_f[None, :] < top_here[:, None], 1.0 / jnp.maximum(top_here, 1.0)[:, None], jnp.float32(0.0)
        )
        at_row = (row_here[:, None] == jnp.arange(positions, dtype=jnp.float32)[None, :]).astype(jnp.float32)
        return (weight[:, :, None] * at_row[:, None, :]).reshape(arrived.shape[0], LEV * positions)

    mixed = jnp.concatenate([mixing(0), mixing(2), mixing(4)], axis=1)
    plume = jnp.dot(
        mixed.T, arrived[:, :det_at], precision=lax.Precision.HIGHEST, preferred_element_type=jnp.float32
    )
    share = LEV * positions

    def injected(group, lo, span):
        part = plume[group * share : (group + 1) * share, lo : lo + PR * span]
        return part.reshape(LEV, positions, PR, span).reshape(LEV, rows, span)

    injection = injected(0, 0, cols)
    left = injected(1, width, h)
    right = injected(2, width + strip, h)
    gap = jnp.zeros((LEV, rows, lanes - cols - 2 * h), jnp.float32)
    band = jnp.concatenate([injection, right, gap, left], axis=2)
    inj = rows_halo(band, h)
    at = {"wx": 2 * levels}
    at["wy"] = at["wx"] + levels
    at["kd"] = at["wy"] + levels
    at["rate"] = at["kd"] + levels - 1

    gi = lax.axis_index("gx")
    gj = lax.axis_index("gy")
    rpos = jnp.arange(rows + 2 * h, dtype=jnp.int32)
    rpos = jnp.where(rpos < rows + h, rpos, rpos - (rows + 2 * h))
    lpos = jnp.arange(lanes, dtype=jnp.int32)
    lpos = jnp.where(lpos < cols + h, lpos, jnp.where(lpos >= lanes - h, lpos - lanes, -(cols * columns + 1)))
    grow = gi * rows + rpos
    gcol = gj * cols + lpos
    valid = (((grow >= 0) & (grow < lax.axis_size("gx") * rows))[:, None] & (
        (gcol >= 0) & (gcol < columns * cols)
    )[None, :]).astype(jnp.float32)

    kernel = lambda *refs: steps_kernel(*refs, levels=levels, at=at)
    return pl.pallas_call(
        kernel,
        out_shape=jax.ShapeDtypeStruct((2, levels, rows, cols), jnp.float32),
        scratch_shapes=[
            pltpu.VMEM((2 * levels, rows + 2 * h, lanes), jnp.float32),
            pltpu.VMEM((levels, rows + 2 * h, lanes), jnp.float32),
            pltpu.VMEM((levels, rows + 2 * h, lanes), jnp.float32),
        ],
    )(ext, inj, valid)


def solution(mesh):
    in_specs = (
        P(None, None, "gx", "gy"),
        P(None, "gx", "gy"),
        P(None, "gx", "gy"),
        P(None, "gx", "gy"),
        P("gx", "gy"),
        P(("gx", "gy"), None),
        P(("gx", "gy")),
        P(("gx", "gy")),
        P(("gx", "gy")),
    )
    out_specs = P(None, None, "gx", "gy")
    return jax.shard_map(
        on_device, mesh=mesh, in_specs=in_specs, out_specs=out_specs, check_vma=False
    )
```

```python
import jax
import jax.numpy as jnp
from jax import lax
from jax.sharding import PartitionSpec as P
from jax.experimental import pallas as pl
from jax.experimental.pallas import tpu as pltpu

LEV = 16
STEPS = 4
PR = 16
CAP = 8
HALO = STEPS


def from_behind(value, axis, steps):
    count = lax.axis_size(axis)
    initial, last = (max(0, -steps), min(count, count - steps))
    return lax.ppermute(value, axis, [(source, source + steps) for source in range(initial, last)])


def rows_halo(band, h):
    r = band.shape[1]
    below = from_behind(band[:, :h], "gx", -1)
    above = from_behind(band[:, r - h :], "gx", 1)
    return jnp.concatenate([band, below, above], axis=1)


def column_halo(a, h):
    c, r, w = a.shape
    left = from_behind(a[:, :, w - h:].reshape(c, r * h), "gy", 1).reshape(c, r, h)
    right = from_behind(a[:, :, :h].reshape(c, r * h), "gy", -1).reshape(c, r, h)
    return left, right


def with_halo(a, left, right, h, lanes):
    c, r, w = a.shape
    gap = jnp.zeros((c, r, lanes - w - 2 * h), a.dtype)
    return rows_halo(jnp.concatenate([a, right, gap, left], axis=2), h)


def steps_kernel(ext_ref, inj_ref, valid_ref, o_ref, q_s, inv_s, sw_s, *, levels, at):
    rows_ext, lanes = valid_ref.shape
    rows, cols = o_ref.shape[2], o_ref.shape[3]
    for p in range(2 * levels):
        q_s[p] = ext_ref[p]
    valid = valid_ref[...] != 0.0
    keep = 1.0 - jnp.exp(-ext_ref[at["rate"]])
    sweep_prev = None
    for l in range(levels):
        diag = jnp.ones((rows_ext, lanes), jnp.float32)
        if l >= 1:
            diag = diag + ext_ref[at["kd"] + l - 1]
        if l < levels - 1:
            diag = diag + ext_ref[at["kd"] + l]
        if l == 0:
            denom = diag
        else:
            denom = diag - (-ext_ref[at["kd"] + l - 1]) * sweep_prev
        inv_here = 1.0 / denom
        inv_s[l] = inv_here
        if l < levels - 1:
            sweep_prev = (-ext_ref[at["kd"] + l]) * inv_here
            sw_s[l] = sweep_prev
    zero = jnp.zeros((rows_ext, lanes), jnp.float32)

    def one_step(step, carry):
        def forward(l, prev):
            p0, p1 = prev
            wxl = ext_ref[at["wx"] + l]
            wyl = ext_ref[at["wy"] + l]
            out_x = jnp.maximum(wxl, 0.0)
            in_x = jnp.minimum(wxl, 0.0)
            out_y = jnp.maximum(wyl, 0.0)
            in_y = jnp.minimum(wyl, 0.0)

            def advect(x):
                flux_x = out_x * x + in_x * pltpu.roll(x, rows_ext - 1, 0)
                flux_y = out_y * x + in_y * pltpu.roll(x, lanes - 1, 1)
                return x - (flux_x - pltpu.roll(flux_x, 1, 0)) - (flux_y - pltpu.roll(flux_y, 1, 1))

            a0 = advect(q_s[l])
            a1 = advect(q_s[levels + l])
            so2 = a0 + inj_ref[l]
            loss = so2 * keep
            c0 = so2 - loss
            c1 = a1 + 1.5 * loss
            inv = inv_s[l]
            lower = -ext_ref[at["kd"] + jnp.maximum(l - 1, 0)]
            f0 = (c0 - lower * p0) * inv
            f1 = (c1 - lower * p1) * inv
            q_s[l] = f0
            q_s[levels + l] = f1
            return (f0, f1)

        f0, f1 = lax.fori_loop(0, levels, forward, (zero, zero), unroll=True)
        q_s[levels - 1] = jnp.where(valid, f0, 0.0)
        q_s[2 * levels - 1] = jnp.where(valid, f1, 0.0)

        def backward(i, nxt):
            l = levels - 2 - i
            n0, n1 = nxt
            sw = sw_s[l]
            r0 = q_s[l] - sw * n0
            r1 = q_s[levels + l] - sw * n1
            q_s[l] = jnp.where(valid, r0, 0.0)
            q_s[levels + l] = jnp.where(valid, r1, 0.0)
            return (r0, r1)

        lax.fori_loop(0, levels - 1, backward, (f0, f1), unroll=True)
        return carry

    lax.fori_loop(0, STEPS, one_step, 0, unroll=True)
    for p in range(2 * levels):
        o_ref[p // levels, p % levels] = q_s[p, 0:rows, 0:cols]


def thomas_factor(kdiff):
    levels = kdiff.shape[0] + 1
    lower = []
    upper = []
    diag = []
    for l in range(levels):
        d_here = jnp.ones_like(kdiff[0])
        if l >= 1:
            d_here = d_here + kdiff[l - 1]
            lower.append(-kdiff[l - 1])
        else:
            lower.append(jnp.zeros_like(kdiff[0]))
        if l < levels - 1:
            d_here = d_here + kdiff[l]
            upper.append(-kdiff[l])
        else:
            upper.append(jnp.zeros_like(kdiff[0]))
        diag.append(d_here)
    inverse = []
    sweep = []
    for l in range(levels):
        if l == 0:
            denom = diag[0]
        else:
            denom = diag[l] - lower[l] * sweep[l - 1]
        inv_here = 1.0 / denom
        inverse.append(inv_here)
        sweep.append(upper[l] * inv_here)
    return (lower, inverse, sweep)


def thomas_solve(rhs, factors):
    lower, inverse, sweep = factors
    levels = len(inverse)
    forward = []
    for l in range(levels):
        if l == 0:
            forward.append(rhs[:, 0] * inverse[0])
        else:
            forward.append((rhs[:, l] - lower[l] * forward[l - 1]) * inverse[l])
    result = [None] * levels
    result[levels - 1] = forward[levels - 1]
    for l in range(levels - 2, -1, -1):
        result[l] = forward[l] - sweep[l] * result[l + 1]
    return jnp.stack(result, axis=1)


def upwind(courant, here, ahead):
    return jnp.maximum(courant, 0.0) * here + jnp.minimum(courant, 0.0) * ahead


def plume_matrix(blocks, row_f, top_f, positions):
    levels = jnp.arange(LEV, dtype=jnp.float32)
    weight = jnp.where(
        levels[None, :] < top_f[:, None], 1.0 / jnp.maximum(top_f, 1.0)[:, None], jnp.float32(0.0)
    )
    place = (row_f[:, None] == jnp.arange(positions, dtype=jnp.float32)[None, :]).astype(
        jnp.float32
    )
    mixed = (weight[:, :, None] * place[:, None, :]).reshape(blocks.shape[0], LEV * positions)
    return jnp.dot(
        mixed.T, blocks, precision=lax.Precision.HIGHEST, preferred_element_type=jnp.float32
    )


def on_device(tracers, wind_x, wind_y, kdiff, rate, seg_blocks, seg_target, seg_row, seg_top):
    rows = tracers.shape[2]
    cols = tracers.shape[3]
    levels = tracers.shape[1]
    positions = rows // PR
    count = seg_target.shape[0]
    width = seg_blocks.shape[1]
    h = HALO
    row_f = seg_row.astype(jnp.float32)
    top_f = seg_top.astype(jnp.float32)
    columns = lax.axis_size("gy")
    order = jnp.arange(count, dtype=jnp.int32)
    same = seg_target[:, None] == seg_target[None, :]
    rank = jnp.sum((same & (order[:, None] < order[None, :])).astype(jnp.int32), axis=0)
    strip = PR * h
    blocks3 = seg_blocks.reshape(count, PR, cols)
    tail = blocks3[:, :, cols - h :].reshape(count, strip)
    head = blocks3[:, :, :h].reshape(count, strip)
    det = jnp.stack([row_f, top_f], axis=1)
    det_at = width + 2 * strip
    wide = det_at + 6

    def pad(x, before, after):
        return jnp.pad(x, ((0, 0), (before, after)))

    payload = jnp.concatenate(
        [
            pad(jnp.concatenate([seg_blocks, pad(det, 2 * strip, 4)], axis=1), 0, 0),
            pad(jnp.concatenate([pad(tail, width, strip), pad(det, 2, 2)], axis=1), 0, 0),
            pad(jnp.concatenate([pad(head, width + strip, 0), pad(det, 4, 0)], axis=1), 0, 0),
        ],
        axis=0,
    )
    dest = jnp.concatenate(
        [seg_target * CAP + rank, (seg_target + 1) * CAP + rank, (seg_target - 1) * CAP + rank]
    )
    place = (dest[:, None] == jnp.arange(columns * CAP, dtype=jnp.int32)[None, :]).astype(
        jnp.float32
    )
    outgoing = jnp.dot(
        place.T, payload, precision=lax.Precision.HIGHEST, preferred_element_type=jnp.float32
    )
    lanes = -(-(cols + 2 * h) // 128) * 128
    packed = jnp.concatenate(
        [tracers.reshape(2 * levels, rows, cols), wind_x, wind_y, kdiff, rate[None]], axis=0
    )
    left_cols, right_cols = column_halo(packed, h)
    sendable, left_cols, right_cols = lax.optimization_barrier(
        (outgoing.reshape(columns, CAP, wide), left_cols, right_cols)
    )
    arrived = lax.all_to_all(
        sendable,
        "gy",
        split_axis=0,
        concat_axis=0,
        tiled=True,
    ).reshape(columns * CAP, wide)

    ext = with_halo(packed, left_cols, right_cols, h, lanes)

    levels_f = jnp.arange(LEV, dtype=jnp.float32)

    def mixing(d):
        row_here = arrived[:, det_at + d]
        top_here = arrived[:, det_at + d + 1]
        weight = jnp.where(
            levels_f[None, :] < top_here[:, None], 1.0 / jnp.maximum(top_here, 1.0)[:, None], jnp.float32(0.0)
        )
        at_row = (row_here[:, None] == jnp.arange(positions, dtype=jnp.float32)[None, :]).astype(jnp.float32)
        return (weight[:, :, None] * at_row[:, None, :]).reshape(arrived.shape[0], LEV * positions)

    mixed = jnp.concatenate([mixing(0), mixing(2), mixing(4)], axis=1)
    plume = jnp.dot(
        mixed.T, arrived[:, :det_at], precision=lax.Precision.HIGHEST, preferred_element_type=jnp.float32
    )
    share = LEV * positions

    def injected(group, lo, span):
        part = plume[group * share : (group + 1) * share, lo : lo + PR * span]
        return part.reshape(LEV, positions, PR, span).reshape(LEV, rows, span)

    injection = injected(0, 0, cols)
    left = injected(1, width, h)
    right = injected(2, width + strip, h)
    gap = jnp.zeros((LEV, rows, lanes - cols - 2 * h), jnp.float32)
    band = jnp.concatenate([injection, right, gap, left], axis=2)
    inj = rows_halo(band, h)
    at = {"wx": 2 * levels}
    at["wy"] = at["wx"] + levels
    at["kd"] = at["wy"] + levels
    at["rate"] = at["kd"] + levels - 1

    gi = lax.axis_index("gx")
    gj = lax.axis_index("gy")
    rpos = jnp.arange(rows + 2 * h, dtype=jnp.int32)
    rpos = jnp.where(rpos < rows + h, rpos, rpos - (rows + 2 * h))
    lpos = jnp.arange(lanes, dtype=jnp.int32)
    lpos = jnp.where(lpos < cols + h, lpos, jnp.where(lpos >= lanes - h, lpos - lanes, -(cols * columns + 1)))
    grow = gi * rows + rpos
    gcol = gj * cols + lpos
    valid = (((grow >= 0) & (grow < lax.axis_size("gx") * rows))[:, None] & (
        (gcol >= 0) & (gcol < columns * cols)
    )[None, :]).astype(jnp.float32)

    kernel = lambda *refs: steps_kernel(*refs, levels=levels, at=at)
    return pl.pallas_call(
        kernel,
        out_shape=jax.ShapeDtypeStruct((2, levels, rows, cols), jnp.float32),
        scratch_shapes=[
            pltpu.VMEM((2 * levels, rows + 2 * h, lanes), jnp.float32),
            pltpu.VMEM((levels, rows + 2 * h, lanes), jnp.float32),
            pltpu.VMEM((levels, rows + 2 * h, lanes), jnp.float32),
        ],
    )(ext, inj, valid)


def solution(mesh):
    in_specs = (
        P(None, None, "gx", "gy"),
        P(None, "gx", "gy"),
        P(None, "gx", "gy"),
        P(None, "gx", "gy"),
        P("gx", "gy"),
        P(("gx", "gy"), None),
        P(("gx", "gy")),
        P(("gx", "gy")),
        P(("gx", "gy")),
    )
    out_specs = P(None, None, "gx", "gy")
    return jax.shard_map(
        on_device, mesh=mesh, in_specs=in_specs, out_specs=out_specs, check_vma=False
    )
```
